512 devices in a mesh: gx: 128 (over x, z, core), gy: 4 (over y).
Axes of the slice: x: 4, y: 4, z: 16, core: 2. Of those that a mesh axis runs over, the one named last changes fastest.
Arguments:
- field: bfloat16 [20, 128, 128, 1024], P(None, 'gx', 'gy'), may hold values from -6 to 6
- cotangent: bfloat16 [20, 128, 128, 1024], P(None, 'gx', 'gy'), may hold values from -6 to 6
- spectral_weight: bfloat16 [2, 20, 20, 24, 4608], P(None, None, None, None, ('gy', 'gx')), may hold values from -30 to 30
- local_weight: bfloat16 [20, 20], replicated, may hold values from -1.25 to 1.25
- bias: float32 [20], replicated, may hold values from -4 to 4
Outputs:
- grad_field: bfloat16 [20, 128, 128, 1024], P(None, 'gx', 'gy')
- grad_weight: float32 [2, 20, 20, 24, 4608], P(None, None, None, None, ('gy', 'gx'))
The draws below stay inside these ranges and needn't reach their ends.
All inputs are finite; a program needn't handle non-finite values.
Results may differ from the reference program's by a relative error of at most 0.03.
Values may be sent and summed in bfloat16 or wider, within the bound.
No kernel may reach another device: no remote copies, remote signals or barrier semaphores. Data moves between devices by JAX's collectives and lax.ppermute only.
A program may use at most 64 MiB of HBM per device.

```python
import math
import jax
import jax.numpy as jnp
from jax import lax

C = 20
NX = 128
NY = 128
NZ = 128
NT = 8
MS = 24
MT = 8


def draw_spectral_weight(key, part):
    scale_key, value_key = jax.random.split(jax.random.fold_in(key, 17))
    shape = (2, C, C, MS, MS * MS * MT)
    logs = jax.random.uniform(scale_key, (MS * MS * MT,), jnp.float32, math.log(0.2), math.log(5.0))
    scales = jnp.exp(logs)
    base = jnp.clip(jax.random.normal(value_key, shape, jnp.float32), -3.0, 3.0)
    return (2.0 * base * scales).astype(jnp.bfloat16)


def level_of(own_key, shape, pieces, low, high):
    factor_of, own = 1.0, jax.random.fold_in(own_key, 6)
    for axis_at, shards_of in pieces:
        heights = jnp.exp(jax.random.uniform(jax.random.fold_in(own, axis_at), (shards_of,), jnp.float32, low / len(pieces), high / len(pieces)))
        factor_of = factor_of * jnp.repeat(heights, shape[axis_at] // shards_of).reshape([-1 if axis == axis_at else 1 for axis in range(len(shape))])
    return factor_of


def bell_draw(key, extent, width, limit, pieces=(), kind=jnp.bfloat16):
    loudness = level_of(key, extent, pieces, -0.22, 0.18) if pieces else 1.0
    values = jax.random.normal(key, extent, jnp.float32) * width * loudness
    return jnp.minimum(jnp.maximum(values, -limit), limit).astype(kind)


def setup_inputs(seed: int = 0) -> dict:
    keys = jax.random.split(jax.random.key(seed), 6)
    field = bell_draw(keys[0], (C, NX, NY, NZ * NT), 1.0, 6.0, ((1, 128), (2, 4)))
    cotangent = bell_draw(keys[1], (C, NX, NY, NZ * NT), 1.0, 6.0, ((1, 128), (2, 4)))
    spectral_weight = draw_spectral_weight(jax.random.fold_in(keys[5], 71), 0)
    local_weight = bell_draw(keys[3], (C, C), C ** -0.5, 1.25)
    bias = bell_draw(keys[4], (C,), 1.0, 4.0, (), jnp.float32)
    return {"field": field, "cotangent": cotangent, "spectral_weight": spectral_weight, "local_weight": local_weight, "bias": bias}


def axis_tables(length, kept_count, positions):
    half_kept = kept_count // 2
    mode_index = jnp.arange(kept_count, dtype=jnp.int32)
    frequency = jnp.where(mode_index < half_kept, mode_index, mode_index - kept_count)
    phases = jnp.mod(frequency[:, None] * positions[None, :].astype(jnp.int32), length)
    angles = phases.astype(jnp.float32) * (2.0 * math.pi / length)
    factor = 1.0 / math.sqrt(length)
    return ((jnp.cos(angles) * factor).astype(jnp.bfloat16), (jnp.sin(angles) * factor).astype(jnp.bfloat16))

def plane_tables(depth_cells, time_steps, kept_count, kept_time):
    period = depth_cells * time_steps
    positions = jnp.arange(period, dtype=jnp.int32)
    depth_pos = positions // time_steps
    time_pos = positions % time_steps
    mode_index = jnp.arange(kept_count * kept_time, dtype=jnp.int32)
    space_index = mode_index // kept_time
    time_index = mode_index % kept_time
    frequency = jnp.where(space_index < kept_count // 2, space_index, space_index - kept_count)
    phase_depth = jnp.mod(depth_pos[:, None] * frequency[None, :], depth_cells)
    phase_time = jnp.mod(time_pos[:, None] * time_index[None, :], time_steps)
    phases = jnp.mod(phase_depth * time_steps + phase_time * depth_cells, period)
    angles = phases.astype(jnp.float32) * (2.0 * math.pi / period)
    factor = 1.0 / math.sqrt(period)
    return jnp.concatenate([jnp.cos(angles) * factor, -jnp.sin(angles) * factor], axis=1).astype(jnp.bfloat16)

def forward_axis(values, cos_table, sin_table):
    values = values.astype(jnp.float32)
    with_cos = jnp.einsum('kn,lnrm->lrkm', cos_table.astype(jnp.float32), values)
    with_sin = jnp.einsum('kn,lnrm->lrkm', sin_table.astype(jnp.float32), values)
    real_part = with_cos[:, 0] + with_sin[:, 1]
    imag_part = with_cos[:, 1] - with_sin[:, 0]
    return jnp.stack([real_part, imag_part], axis=1)

def inverse_axis(values, cos_table, sin_table):
    values = values.astype(jnp.float32)
    with_cos = jnp.einsum('kn,lrkm->lnrm', cos_table.astype(jnp.float32), values)
    with_sin = jnp.einsum('kn,lrkm->lnrm', sin_table.astype(jnp.float32), values)
    real_part = with_cos[:, :, 0] - with_sin[:, :, 1]
    imag_part = with_cos[:, :, 1] + with_sin[:, :, 0]
    return jnp.stack([real_part, imag_part], axis=2)

def spectral_apply(weights, mode_values):
    real_weight = weights[0].astype(jnp.float32)
    imag_weight = weights[1].astype(jnp.float32)
    real_mode = mode_values[:, 0].astype(jnp.float32)
    imag_mode = mode_values[:, 1].astype(jnp.float32)
    out_real = jnp.einsum('iokm,ikm->okm', real_weight, real_mode) - jnp.einsum('iokm,ikm->okm', imag_weight, imag_mode)
    out_imag = jnp.einsum('iokm,ikm->okm', real_weight, imag_mode) + jnp.einsum('iokm,ikm->okm', imag_weight, real_mode)
    return jnp.stack([out_real, out_imag], axis=1).astype(jnp.bfloat16)

def spectral_adjoint(weights, mode_values, upstream_modes):
    real_weight = weights[0].astype(jnp.float32)
    imag_weight = weights[1].astype(jnp.float32)
    real_mode = mode_values[:, 0].astype(jnp.float32)
    imag_mode = mode_values[:, 1].astype(jnp.float32)
    real_up = upstream_modes[:, 0].astype(jnp.float32)
    imag_up = upstream_modes[:, 1].astype(jnp.float32)
    grad_real = real_up[None] * real_mode[:, None] + imag_up[None] * imag_mode[:, None]
    grad_imag = imag_up[None] * real_mode[:, None] - real_up[None] * imag_mode[:, None]
    back_real = jnp.einsum('iokm,okm->ikm', real_weight, real_up) + jnp.einsum('iokm,okm->ikm', imag_weight, imag_up)
    back_imag = jnp.einsum('iokm,okm->ikm', real_weight, imag_up) - jnp.einsum('iokm,okm->ikm', imag_weight, real_up)
    return (jnp.stack([grad_real, grad_imag], axis=0), jnp.stack([back_real, back_imag], axis=1))

def gelu_slope(values):
    return 0.5 * (1.0 + lax.erf(values * 0.7071067811865476)) + values * jnp.exp(-0.5 * values * values) * 0.3989422804014327

def reference(field, cotangent, spectral_weight, local_weight, bias):
    kept_plane = MS * MT
    plane_table = plane_tables(NZ, NT, MS, MT)
    cos_wide, sin_wide = axis_tables(NY, MS, jnp.arange(NY, dtype=jnp.int32))
    cos_across, sin_across = axis_tables(NX, MS, jnp.arange(NX, dtype=jnp.int32))
    local_float = local_weight.astype(jnp.float32)

    def first_step(planes):
        product = jnp.dot(planes.reshape(-1, NZ * NT), plane_table, preferred_element_type=jnp.float32)
        return product.astype(jnp.bfloat16)

    def forward_chain(moved):
        coeffs = lax.map(first_step, moved).reshape(NX * C, NY, 2, kept_plane)
        row_modes = forward_axis(coeffs, cos_wide, sin_wide).astype(jnp.bfloat16)
        row_modes = row_modes.reshape(NX, C, 2, MS * kept_plane).transpose(1, 0, 2, 3)
        return forward_axis(row_modes, cos_across, sin_across).astype(jnp.bfloat16)

    def inverse_chain(mode_values):
        across = inverse_axis(mode_values, cos_across, sin_across).astype(jnp.bfloat16)
        row_modes = across.transpose(1, 0, 2, 3).reshape(NX * C, 2, MS, kept_plane)
        cell_modes = inverse_axis(row_modes, cos_wide, sin_wide).astype(jnp.bfloat16)
        return cell_modes.reshape(NX, C * NY, 2 * kept_plane)

    def last_step(cell_modes):
        summed = lax.dot_general(cell_modes, plane_table, (((1,), (1,)), ((), ())), preferred_element_type=jnp.float32)
        return summed.reshape(C, NY, NZ * NT)
    moved_field = jnp.moveaxis(field, 1, 0)
    moved_cot = jnp.moveaxis(cotangent, 1, 0)
    field_modes = forward_chain(moved_field)
    mixed_modes = spectral_apply(spectral_weight, field_modes)
    joined = inverse_chain(mixed_modes)

    def activate(inputs):
        cell_modes, planes, cot_planes = inputs
        direct = jnp.einsum('io,iyp->oyp', local_float, planes.astype(jnp.float32))
        before = last_step(cell_modes) + direct + bias.astype(jnp.float32)[:, None, None]
        return (cot_planes.astype(jnp.float32) * gelu_slope(before)).astype(jnp.bfloat16)
    upstream = lax.map(activate, (joined, moved_field, moved_cot))
    upstream_modes = forward_chain(upstream)
    grad_weight, back_modes = spectral_adjoint(spectral_weight, field_modes, upstream_modes)
    back_joined = inverse_chain(back_modes.astype(jnp.bfloat16))

    def finish(inputs):
        cell_modes, up_planes = inputs
        direct = jnp.einsum('io,oyp->iyp', local_float, up_planes.astype(jnp.float32))
        return (last_step(cell_modes) + direct).astype(jnp.bfloat16)
    result = lax.map(finish, (back_joined, upstream))
    return (jnp.moveaxis(result, 0, 1), grad_weight)
```

```python
import math

import jax
import jax.numpy as jnp
from jax import lax
from jax.sharding import PartitionSpec as P

NX = 128
NY = 128
NZ = 128
NT = 8
MS = 24
MT = 8


def axis_tables(length, kept_count, positions):
    half_kept = kept_count // 2
    mode_index = jnp.arange(kept_count, dtype=jnp.int32)
    frequency = jnp.where(mode_index < half_kept, mode_index, mode_index - kept_count)
    phases = jnp.mod(frequency[:, None] * positions[None, :], length)
    angles = phases.astype(jnp.float32) * (2.0 * math.pi / length)
    factor = 1.0 / math.sqrt(length)
    return (
        (jnp.cos(angles) * factor).astype(jnp.bfloat16),
        (jnp.sin(angles) * factor).astype(jnp.bfloat16),
    )


def plane_tables(depth_cells, time_steps, kept_count, kept_time):
    period = depth_cells * time_steps
    positions = jnp.arange(period, dtype=jnp.int32)
    depth_pos = positions // time_steps
    time_pos = positions % time_steps
    mode_index = jnp.arange(kept_count * kept_time, dtype=jnp.int32)
    space_index = mode_index // kept_time
    time_index = mode_index % kept_time
    frequency = jnp.where(space_index < kept_count // 2, space_index, space_index - kept_count)
    phase_depth = jnp.mod(depth_pos[:, None] * frequency[None, :], depth_cells)
    phase_time = jnp.mod(time_pos[:, None] * time_index[None, :], time_steps)
    phases = jnp.mod(phase_depth * time_steps + phase_time * depth_cells, period)
    angles = phases.astype(jnp.float32) * (2.0 * math.pi / period)
    factor = 1.0 / math.sqrt(period)
    return jnp.concatenate([jnp.cos(angles) * factor, -jnp.sin(angles) * factor], axis=1).astype(
        jnp.bfloat16
    )


def forward_axis(values, cos_table, sin_table):
    with_cos = jnp.einsum("kn,lnrm->lrkm", cos_table, values, preferred_element_type=jnp.float32)
    with_sin = jnp.einsum("kn,lnrm->lrkm", sin_table, values, preferred_element_type=jnp.float32)
    real_part = with_cos[:, 0] + with_sin[:, 1]
    imag_part = with_cos[:, 1] - with_sin[:, 0]
    return jnp.stack([real_part, imag_part], axis=1)


def inverse_axis(values, cos_table, sin_table):
    with_cos = jnp.einsum("kn,lrkm->lnrm", cos_table, values, preferred_element_type=jnp.float32)
    with_sin = jnp.einsum("kn,lrkm->lnrm", sin_table, values, preferred_element_type=jnp.float32)
    real_part = with_cos[:, :, 0] - with_sin[:, :, 1]
    imag_part = with_cos[:, :, 1] + with_sin[:, :, 0]
    return jnp.stack([real_part, imag_part], axis=2)


def spectral_apply(weights, mode_values):
    real_weight, imag_weight = (weights[0], weights[1])
    real_mode, imag_mode = (mode_values[:, 0], mode_values[:, 1])
    out_real = jnp.einsum(
        "iokm,ikm->okm", real_weight, real_mode, preferred_element_type=jnp.float32
    ) - jnp.einsum("iokm,ikm->okm", imag_weight, imag_mode, preferred_element_type=jnp.float32)
    out_imag = jnp.einsum(
        "iokm,ikm->okm", real_weight, imag_mode, preferred_element_type=jnp.float32
    ) + jnp.einsum("iokm,ikm->okm", imag_weight, real_mode, preferred_element_type=jnp.float32)
    return jnp.stack([out_real, out_imag], axis=1).astype(jnp.bfloat16)


def spectral_adjoint(weights, mode_values, upstream_modes):
    real_weight, imag_weight = (weights[0], weights[1])
    real_mode = mode_values[:, 0].astype(jnp.float32)
    imag_mode = mode_values[:, 1].astype(jnp.float32)
    real_up = upstream_modes[:, 0].astype(jnp.float32)
    imag_up = upstream_modes[:, 1].astype(jnp.float32)
    grad_real = real_up[None] * real_mode[:, None] + imag_up[None] * imag_mode[:, None]
    grad_imag = imag_up[None] * real_mode[:, None] - real_up[None] * imag_mode[:, None]
    real_low = upstream_modes[:, 0]
    imag_low = upstream_modes[:, 1]
    back_real = jnp.einsum(
        "iokm,okm->ikm", real_weight, real_low, preferred_element_type=jnp.float32
    ) + jnp.einsum("iokm,okm->ikm", imag_weight, imag_low, preferred_element_type=jnp.float32)
    back_imag = jnp.einsum(
        "iokm,okm->ikm", real_weight, imag_low, preferred_element_type=jnp.float32
    ) - jnp.einsum("iokm,okm->ikm", imag_weight, real_low, preferred_element_type=jnp.float32)
    return (jnp.stack([grad_real, grad_imag], axis=0), jnp.stack([back_real, back_imag], axis=1))


def gelu_slope(values):
    return (
        0.5 * (1.0 + lax.erf(values * 0.7071067811865476))
        + values * jnp.exp(-0.5 * values * values) * 0.3989422804014327
    )


def local(field, cotangent, spectral_weight, local_weight, bias):
    channels, width_x, width_y, depth_cells = field.shape
    kept_plane = MS * MT
    plane_table = plane_tables(NZ, NT, MS, MT)
    local_rows = lax.axis_index("gy") * width_y + jnp.arange(width_y, dtype=jnp.int32)
    cos_local, sin_local = axis_tables(NY, MS, local_rows)
    cos_across, sin_across = axis_tables(NX, MS, jnp.arange(NX, dtype=jnp.int32))

    def forward_chain(planes):
        coeffs = jnp.dot(
            planes.reshape(-1, depth_cells), plane_table, preferred_element_type=jnp.float32
        )
        coeffs = coeffs.astype(jnp.bfloat16).reshape(channels * width_x, width_y, 2, kept_plane)
        partial_terms = forward_axis(coeffs, cos_local, sin_local).astype(jnp.bfloat16)
        groups = lax.axis_size("gy")
        lead, parts, kept_rows, plane = partial_terms.shape
        pieces = partial_terms.reshape(lead, parts, groups, kept_rows // groups, plane)
        pieces = lax.all_to_all(pieces, "gy", split_axis=2, concat_axis=2, tiled=True)
        row_modes = jnp.sum(pieces.astype(jnp.float32), axis=2).astype(jnp.bfloat16)
        row_modes = row_modes.reshape(channels, width_x, 2, -1)
        blocks = lax.all_to_all(row_modes, "gx", split_axis=3, concat_axis=1, tiled=True)
        return forward_axis(blocks, cos_across, sin_across).astype(jnp.bfloat16)

    def inverse_chain(mode_values):
        across = inverse_axis(mode_values, cos_across, sin_across).astype(jnp.bfloat16)
        row_modes = lax.all_to_all(across, "gx", split_axis=1, concat_axis=3, tiled=True)
        row_modes = row_modes.reshape(channels * width_x, 2, -1, kept_plane)
        all_rows = lax.all_gather(row_modes, "gy", axis=2, tiled=True)
        cell_modes = inverse_axis(all_rows, cos_local, sin_local).astype(jnp.bfloat16)
        flattened = cell_modes.reshape(-1, 2 * kept_plane)
        summed = lax.dot_general(
            flattened, plane_table, (((1,), (1,)), ((), ())), preferred_element_type=jnp.float32
        )
        return summed.reshape(field.shape)

    field_modes = forward_chain(field)
    mixed_modes = spectral_apply(spectral_weight, field_modes)
    spectral = inverse_chain(mixed_modes)
    direct = jnp.einsum("io,ixyp->oxyp", local_weight, field, preferred_element_type=jnp.float32)
    before = spectral + direct + bias[:, None, None, None]
    upstream = (cotangent.astype(jnp.float32) * gelu_slope(before)).astype(jnp.bfloat16)
    upstream_modes = forward_chain(upstream)
    grad_weight, back_modes = spectral_adjoint(spectral_weight, field_modes, upstream_modes)
    returned = inverse_chain(back_modes.astype(jnp.bfloat16))
    direct_back = jnp.einsum(
        "io,oxyp->ixyp", local_weight, upstream, preferred_element_type=jnp.float32
    )
    return ((returned + direct_back).astype(jnp.bfloat16), grad_weight)


def solution(mesh):
    in_specs = (
        P(None, "gx", "gy", None),
        P(None, "gx", "gy", None),
        P(None, None, None, None, ("gy", "gx")),
        P(),
        P(),
    )
    out_specs = (P(None, "gx", "gy", None), P(None, None, None, None, ("gy", "gx")))
    return jax.shard_map(local, mesh=mesh, in_specs=in_specs, out_specs=out_specs, check_vma=False)
```

```python
import math

import jax
import jax.numpy as jnp
from jax import lax
from jax.sharding import PartitionSpec as P

NX = 128
NY = 128
NZ = 128
NT = 8
MS = 24
MT = 8


def axis_tables(length, kept_count, positions):
    half_kept = kept_count // 2
    mode_index = jnp.arange(kept_count, dtype=jnp.int32)
    frequency = jnp.where(mode_index < half_kept, mode_index, mode_index - kept_count)
    phases = jnp.mod(frequency[:, None] * positions[None, :], length)
    angles = phases.astype(jnp.float32) * (2.0 * math.pi / length)
    factor = 1.0 / math.sqrt(length)
    return (
        (jnp.cos(angles) * factor).astype(jnp.bfloat16),
        (jnp.sin(angles) * factor).astype(jnp.bfloat16),
    )


def plane_tables(depth_cells, time_steps, kept_count, kept_time):
    period = depth_cells * time_steps
    positions = jnp.arange(period, dtype=jnp.int32)
    depth_pos = positions // time_steps
    time_pos = positions % time_steps
    mode_index = jnp.arange(kept_count * kept_time, dtype=jnp.int32)
    space_index = mode_index // kept_time
    time_index = mode_index % kept_time
    frequency = jnp.where(space_index < kept_count // 2, space_index, space_index - kept_count)
    phase_depth = jnp.mod(depth_pos[:, None] * frequency[None, :], depth_cells)
    phase_time = jnp.mod(time_pos[:, None] * time_index[None, :], time_steps)
    phases = jnp.mod(phase_depth * time_steps + phase_time * depth_cells, period)
    angles = phases.astype(jnp.float32) * (2.0 * math.pi / period)
    factor = 1.0 / math.sqrt(period)
    return jnp.concatenate([jnp.cos(angles) * factor, -jnp.sin(angles) * factor], axis=1).astype(
        jnp.bfloat16
    )


def forward_axis(values, cos_table, sin_table):
    with_cos = jnp.einsum("kn,lnrm->lrkm", cos_table, values, preferred_element_type=jnp.float32)
    with_sin = jnp.einsum("kn,lnrm->lrkm", sin_table, values, preferred_element_type=jnp.float32)
    real_part = with_cos[:, 0] + with_sin[:, 1]
    imag_part = with_cos[:, 1] - with_sin[:, 0]
    return jnp.stack([real_part, imag_part], axis=1)


def inverse_axis(values, cos_table, sin_table):
    with_cos = jnp.einsum("kn,lrkm->lnrm", cos_table, values, preferred_element_type=jnp.float32)
    with_sin = jnp.einsum("kn,lrkm->lnrm", sin_table, values, preferred_element_type=jnp.float32)
    real_part = with_cos[:, :, 0] - with_sin[:, :, 1]
    imag_part = with_cos[:, :, 1] + with_sin[:, :, 0]
    return jnp.stack([real_part, imag_part], axis=2)


def spectral_apply(weights, mode_values):
    real_weight, imag_weight = (weights[0], weights[1])
    real_mode, imag_mode = (mode_values[:, 0], mode_values[:, 1])
    out_real = jnp.einsum(
        "iokm,ikm->okm", real_weight, real_mode, preferred_element_type=jnp.float32
    ) - jnp.einsum("iokm,ikm->okm", imag_weight, imag_mode, preferred_element_type=jnp.float32)
    out_imag = jnp.einsum(
        "iokm,ikm->okm", real_weight, imag_mode, preferred_element_type=jnp.float32
    ) + jnp.einsum("iokm,ikm->okm", imag_weight, real_mode, preferred_element_type=jnp.float32)
    return jnp.stack([out_real, out_imag], axis=1).astype(jnp.bfloat16)


def spectral_adjoint(weights, mode_values, upstream_modes):
    real_weight, imag_weight = (weights[0], weights[1])
    real_mode = mode_values[:, 0].astype(jnp.float32)
    imag_mode = mode_values[:, 1].astype(jnp.float32)
    real_up = upstream_modes[:, 0].astype(jnp.float32)
    imag_up = upstream_modes[:, 1].astype(jnp.float32)
    grad_real = real_up[None] * real_mode[:, None] + imag_up[None] * imag_mode[:, None]
    grad_imag = imag_up[None] * real_mode[:, None] - real_up[None] * imag_mode[:, None]
    real_low = upstream_modes[:, 0]
    imag_low = upstream_modes[:, 1]
    back_real = jnp.einsum(
        "iokm,okm->ikm", real_weight, real_low, preferred_element_type=jnp.float32
    ) + jnp.einsum("iokm,okm->ikm", imag_weight, imag_low, preferred_element_type=jnp.float32)
    back_imag = jnp.einsum(
        "iokm,okm->ikm", real_weight, imag_low, preferred_element_type=jnp.float32
    ) - jnp.einsum("iokm,okm->ikm", imag_weight, real_low, preferred_element_type=jnp.float32)
    return (jnp.stack([grad_real, grad_imag], axis=0), jnp.stack([back_real, back_imag], axis=1))


def gelu_slope(values):
    return (
        0.5 * (1.0 + lax.erf(values * 0.7071067811865476))
        + values * jnp.exp(-0.5 * values * values) * 0.3989422804014327
    )


def local(field, cotangent, spectral_weight, local_weight, bias):
    channels, width_x, width_y, depth_cells = field.shape
    kept_plane = MS * MT
    plane_table = plane_tables(NZ, NT, MS, MT)
    local_rows = lax.axis_index("gy") * width_y + jnp.arange(width_y, dtype=jnp.int32)
    cos_local, sin_local = axis_tables(NY, MS, local_rows)
    cos_across, sin_across = axis_tables(NX, MS, jnp.arange(NX, dtype=jnp.int32))

    def forward_chain(planes):
        coeffs = jnp.dot(
            planes.reshape(-1, depth_cells), plane_table, preferred_element_type=jnp.float32
        )
        coeffs = coeffs.astype(jnp.bfloat16).reshape(channels * width_x, width_y, 2, kept_plane)
        partial_terms = forward_axis(coeffs, cos_local, sin_local).astype(jnp.bfloat16)
        groups = lax.axis_size("gy")
        lead, parts, kept_rows, plane = partial_terms.shape
        pieces = partial_terms.reshape(lead, parts, groups, kept_rows // groups, plane)
        pieces = lax.all_to_all(pieces, "gy", split_axis=2, concat_axis=2, tiled=True)
        row_modes = jnp.sum(pieces.astype(jnp.float32), axis=2).astype(jnp.bfloat16)
        row_modes = row_modes.reshape(channels, width_x, 2, -1)
        blocks = lax.all_to_all(row_modes, "gx", split_axis=3, concat_axis=1, tiled=True)
        return forward_axis(blocks, cos_across, sin_across).astype(jnp.bfloat16)

    def inverse_chain(mode_values):
        across = inverse_axis(mode_values, cos_across, sin_across).astype(jnp.bfloat16)
        row_modes = lax.all_to_all(across, "gx", split_axis=1, concat_axis=3, tiled=True)
        row_modes = row_modes.reshape(channels * width_x, 2, -1, kept_plane)
        groups = lax.axis_size("gy")
        lead, parts, kept_rows, plane = row_modes.shape
        copies = jnp.broadcast_to(row_modes[:, :, None], (lead, parts, groups, kept_rows, plane))
        all_rows = lax.all_to_all(copies, "gy", split_axis=2, concat_axis=2, tiled=True)
        all_rows = all_rows.reshape(lead, parts, groups * kept_rows, plane)
        cell_modes = inverse_axis(all_rows, cos_local, sin_local).astype(jnp.bfloat16)
        flattened = cell_modes.reshape(-1, 2 * kept_plane)
        summed = lax.dot_general(
            flattened, plane_table, (((1,), (1,)), ((), ())), preferred_element_type=jnp.float32
        )
        return summed.reshape(field.shape)

    field_modes = forward_chain(field)
    mixed_modes = spectral_apply(spectral_weight, field_modes)
    spectral = inverse_chain(mixed_modes)
    direct = jnp.einsum("io,ixyp->oxyp", local_weight, field, preferred_element_type=jnp.float32)
    before = spectral + direct + bias[:, None, None, None]
    upstream = (cotangent.astype(jnp.float32) * gelu_slope(before)).astype(jnp.bfloat16)
    upstream_modes = forward_chain(upstream)
    grad_weight, back_modes = spectral_adjoint(spectral_weight, field_modes, upstream_modes)
    returned = inverse_chain(back_modes.astype(jnp.bfloat16))
    direct_back = jnp.einsum(
        "io,oxyp->ixyp", local_weight, upstream, preferred_element_type=jnp.float32
    )
    return ((returned + direct_back).astype(jnp.bfloat16), grad_weight)


def solution(mesh):
    in_specs = (
        P(None, "gx", "gy", None),
        P(None, "gx", "gy", None),
        P(None, None, None, None, ("gy", "gx")),
        P(),
        P(),
    )
    out_specs = (P(None, "gx", "gy", None), P(None, None, None, None, ("gy", "gx")))
    return jax.shard_map(local, mesh=mesh, in_specs=in_specs, out_specs=out_specs, check_vma=False)
```

```python
import math

import jax
import jax.numpy as jnp
from jax import lax
from jax.sharding import PartitionSpec as P

NX = 128
NY = 128
NZ = 128
NT = 8
MS = 24
MT = 8


def axis_tables(length, kept_count, positions):
    half_kept = kept_count // 2
    mode_index = jnp.arange(kept_count, dtype=jnp.int32)
    frequency = jnp.where(mode_index < half_kept, mode_index, mode_index - kept_count)
    phases = jnp.mod(frequency[:, None] * positions[None, :], length)
    angles = phases.astype(jnp.float32) * (2.0 * math.pi / length)
    factor = 1.0 / math.sqrt(length)
    return (
        (jnp.cos(angles) * factor).astype(jnp.bfloat16),
        (jnp.sin(angles) * factor).astype(jnp.bfloat16),
    )


def plane_tables(depth_cells, time_steps, kept_count, kept_time):
    period = depth_cells * time_steps
    depth_cos, depth_sin = axis_tables_f32(depth_cells, kept_count, jnp.arange(depth_cells, dtype=jnp.int32))
    time_cos, time_sin = axis_tables_f32(time_steps, kept_time, jnp.arange(time_steps, dtype=jnp.int32), centred=False)
    cos_sum = depth_cos.T[:, None, :, None] * time_cos.T[None, :, None, :] - (
        depth_sin.T[:, None, :, None] * time_sin.T[None, :, None, :]
    )
    sin_sum = depth_sin.T[:, None, :, None] * time_cos.T[None, :, None, :] + (
        depth_cos.T[:, None, :, None] * time_sin.T[None, :, None, :]
    )
    factor = 1.0 / math.sqrt(period)
    shape = (period, kept_count * kept_time)
    return jnp.concatenate(
        [(cos_sum * factor).reshape(shape), (-sin_sum * factor).reshape(shape)], axis=1
    ).astype(jnp.bfloat16)


def axis_tables_f32(length, kept_count, positions, centred=True):
    mode_index = jnp.arange(kept_count, dtype=jnp.int32)
    if centred:
        frequency = jnp.where(mode_index < kept_count // 2, mode_index, mode_index - kept_count)
    else:
        frequency = mode_index
    phases = jnp.mod(frequency[:, None] * positions[None, :], length)
    angles = phases.astype(jnp.float32) * (2.0 * math.pi / length)
    return jnp.cos(angles), jnp.sin(angles)


def forward_axis(values, cos_table, sin_table):
    with_cos = jnp.einsum("kn,lnrm->lrkm", cos_table, values, preferred_element_type=jnp.float32)
    with_sin = jnp.einsum("kn,lnrm->lrkm", sin_table, values, preferred_element_type=jnp.float32)
    real_part = with_cos[:, 0] + with_sin[:, 1]
    imag_part = with_cos[:, 1] - with_sin[:, 0]
    return jnp.stack([real_part, imag_part], axis=1)


def inverse_axis(values, cos_table, sin_table):
    with_cos = jnp.einsum("kn,lrkm->lnrm", cos_table, values, preferred_element_type=jnp.float32)
    with_sin = jnp.einsum("kn,lrkm->lnrm", sin_table, values, preferred_element_type=jnp.float32)
    real_part = with_cos[:, :, 0] - with_sin[:, :, 1]
    imag_part = with_cos[:, :, 1] + with_sin[:, :, 0]
    return jnp.stack([real_part, imag_part], axis=2)


def spectral_apply(weights, mode_values):
    real_weight, imag_weight = (weights[0], weights[1])
    real_mode, imag_mode = (mode_values[:, 0], mode_values[:, 1])
    out_real = jnp.einsum(
        "iokm,ikm->okm", real_weight, real_mode, preferred_element_type=jnp.float32
    ) - jnp.einsum("iokm,ikm->okm", imag_weight, imag_mode, preferred_element_type=jnp.float32)
    out_imag = jnp.einsum(
        "iokm,ikm->okm", real_weight, imag_mode, preferred_element_type=jnp.float32
    ) + jnp.einsum("iokm,ikm->okm", imag_weight, real_mode, preferred_element_type=jnp.float32)
    return jnp.stack([out_real, out_imag], axis=1).astype(jnp.bfloat16)


def spectral_adjoint(weights, mode_values, upstream_modes):
    real_weight, imag_weight = (weights[0], weights[1])
    real_mode = mode_values[:, 0].astype(jnp.float32)
    imag_mode = mode_values[:, 1].astype(jnp.float32)
    real_up = upstream_modes[:, 0].astype(jnp.float32)
    imag_up = upstream_modes[:, 1].astype(jnp.float32)
    grad_real = real_up[None] * real_mode[:, None] + imag_up[None] * imag_mode[:, None]
    grad_imag = imag_up[None] * real_mode[:, None] - real_up[None] * imag_mode[:, None]
    real_low = upstream_modes[:, 0]
    imag_low = upstream_modes[:, 1]
    back_real = jnp.einsum(
        "iokm,okm->ikm", real_weight, real_low, preferred_element_type=jnp.float32
    ) + jnp.einsum("iokm,okm->ikm", imag_weight, imag_low, preferred_element_type=jnp.float32)
    back_imag = jnp.einsum(
        "iokm,okm->ikm", real_weight, imag_low, preferred_element_type=jnp.float32
    ) - jnp.einsum("iokm,okm->ikm", imag_weight, real_low, preferred_element_type=jnp.float32)
    return (jnp.stack([grad_real, grad_imag], axis=0), jnp.stack([back_real, back_imag], axis=1))


def gelu_slope(values):
    return (
        0.5 * (1.0 + lax.erf(values * 0.7071067811865476))
        + values * jnp.exp(-0.5 * values * values) * 0.3989422804014327
    )


def local(field, cotangent, spectral_weight, local_weight, bias):
    channels, width_x, width_y, depth_cells = field.shape
    kept_plane = MS * MT
    plane_table = plane_tables(NZ, NT, MS, MT)
    local_rows = lax.axis_index("gy") * width_y + jnp.arange(width_y, dtype=jnp.int32)
    cos_local, sin_local = axis_tables(NY, MS, local_rows)
    cos_across, sin_across = axis_tables(NX, MS, jnp.arange(NX, dtype=jnp.int32))

    def forward_chain(planes):
        coeffs = jnp.dot(
            planes.reshape(-1, depth_cells), plane_table, preferred_element_type=jnp.float32
        )
        coeffs = coeffs.astype(jnp.bfloat16).reshape(channels * width_x, width_y, 2, kept_plane)
        partial_terms = forward_axis(coeffs, cos_local, sin_local).astype(jnp.bfloat16)
        groups = lax.axis_size("gy")
        lead, parts, kept_rows, plane = partial_terms.shape
        pieces = partial_terms.reshape(lead, parts, groups, kept_rows // groups, plane)
        pieces = lax.all_to_all(pieces, "gy", split_axis=2, concat_axis=2, tiled=True)
        row_modes = jnp.sum(pieces.astype(jnp.float32), axis=2).astype(jnp.bfloat16)
        row_modes = row_modes.reshape(channels, width_x, 2, -1)
        blocks = lax.all_to_all(row_modes, "gx", split_axis=3, concat_axis=1, tiled=True)
        return forward_axis(blocks, cos_across, sin_across).astype(jnp.bfloat16)

    def inverse_chain(mode_values):
        across = inverse_axis(mode_values, cos_across, sin_across).astype(jnp.bfloat16)
        row_modes = lax.all_to_all(across, "gx", split_axis=1, concat_axis=3, tiled=True)
        row_modes = row_modes.reshape(channels * width_x, 2, -1, kept_plane)
        all_rows = lax.all_gather(row_modes, "gy", axis=2, tiled=True)
        cell_modes = inverse_axis(all_rows, cos_local, sin_local).astype(jnp.bfloat16)
        flattened = cell_modes.reshape(-1, 2 * kept_plane)
        summed = lax.dot_general(
            flattened, plane_table, (((1,), (1,)), ((), ())), preferred_element_type=jnp.float32
        )
        return summed.reshape(field.shape)

    field_modes = forward_chain(field)
    mixed_modes = spectral_apply(spectral_weight, field_modes)
    spectral = inverse_chain(mixed_modes)
    direct = jnp.einsum("io,ixyp->oxyp", local_weight, field, preferred_element_type=jnp.float32)
    before = spectral + direct + bias[:, None, None, None]
    upstream = (cotangent.astype(jnp.float32) * gelu_slope(before)).astype(jnp.bfloat16)
    upstream_modes = forward_chain(upstream)
    grad_weight, back_modes = spectral_adjoint(spectral_weight, field_modes, upstream_modes)
    returned = inverse_chain(back_modes.astype(jnp.bfloat16))
    direct_back = jnp.einsum(
        "io,oxyp->ixyp", local_weight, upstream, preferred_element_type=jnp.float32
    )
    return ((returned + direct_back).astype(jnp.bfloat16), grad_weight)


def solution(mesh):
    in_specs = (
        P(None, "gx", "gy", None),
        P(None, "gx", "gy", None),
        P(None, None, None, None, ("gy", "gx")),
        P(),
        P(),
    )
    out_specs = (P(None, "gx", "gy", None), P(None, None, None, None, ("gy", "gx")))
    return jax.shard_map(local, mesh=mesh, in_specs=in_specs, out_specs=out_specs, check_vma=False)
```

```python
import math

import jax
import jax.numpy as jnp
from jax import lax
from jax.sharding import PartitionSpec as P

NX = 128
NY = 128
NZ = 128
NT = 8
MS = 24
MT = 8


def axis_tables(length, kept_count, positions):
    half_kept = kept_count // 2
    mode_index = jnp.arange(kept_count, dtype=jnp.int32)
    frequency = jnp.where(mode_index < half_kept, mode_index, mode_index - kept_count)
    phases = jnp.mod(frequency[:, None] * positions[None, :], length)
    angles = phases.astype(jnp.float32) * (2.0 * math.pi / length)
    factor = 1.0 / math.sqrt(length)
    return (
        (jnp.cos(angles) * factor).astype(jnp.bfloat16),
        (jnp.sin(angles) * factor).astype(jnp.bfloat16),
    )


def plane_tables(depth_cells, time_steps, kept_count, kept_time):
    period = depth_cells * time_steps
    positions = jnp.arange(period, dtype=jnp.int32)
    depth_pos = positions // time_steps
    time_pos = positions % time_steps
    mode_index = jnp.arange(kept_count * kept_time, dtype=jnp.int32)
    space_index = mode_index // kept_time
    time_index = mode_index % kept_time
    frequency = jnp.where(space_index < kept_count // 2, space_index, space_index - kept_count)
    phase_depth = jnp.mod(depth_pos[:, None] * frequency[None, :], depth_cells)
    phase_time = jnp.mod(time_pos[:, None] * time_index[None, :], time_steps)
    phases = jnp.mod(phase_depth * time_steps + phase_time * depth_cells, period)
    angles = phases.astype(jnp.float32) * (2.0 * math.pi / period)
    factor = 1.0 / math.sqrt(period)
    return jnp.concatenate([jnp.cos(angles) * factor, -jnp.sin(angles) * factor], axis=1).astype(
        jnp.bfloat16
    )


def forward_axis(values, cos_table, sin_table):
    table = jnp.stack(
        [jnp.stack([cos_table, sin_table], axis=1), jnp.stack([-sin_table, cos_table], axis=1)], axis=0
    )
    return jnp.einsum("pkrn,lnrm->lpkm", table, values, preferred_element_type=jnp.float32)


def inverse_axis(values, cos_table, sin_table):
    table = jnp.stack(
        [jnp.stack([cos_table, -sin_table], axis=0), jnp.stack([sin_table, cos_table], axis=0)], axis=0
    )
    return jnp.einsum("rpkn,lpkm->lnrm", table, values, preferred_element_type=jnp.float32)


def spectral_apply(weights, mode_values):
    real_weight, imag_weight = (weights[0], weights[1])
    real_mode, imag_mode = (mode_values[:, 0], mode_values[:, 1])
    out_real = jnp.einsum(
        "iokm,ikm->okm", real_weight, real_mode, preferred_element_type=jnp.float32
    ) - jnp.einsum("iokm,ikm->okm", imag_weight, imag_mode, preferred_element_type=jnp.float32)
    out_imag = jnp.einsum(
        "iokm,ikm->okm", real_weight, imag_mode, preferred_element_type=jnp.float32
    ) + jnp.einsum("iokm,ikm->okm", imag_weight, real_mode, preferred_element_type=jnp.float32)
    return jnp.stack([out_real, out_imag], axis=1).astype(jnp.bfloat16)


def spectral_adjoint(weights, mode_values, upstream_modes):
    real_weight, imag_weight = (weights[0], weights[1])
    real_mode = mode_values[:, 0].astype(jnp.float32)
    imag_mode = mode_values[:, 1].astype(jnp.float32)
    real_up = upstream_modes[:, 0].astype(jnp.float32)
    imag_up = upstream_modes[:, 1].astype(jnp.float32)
    grad_real = real_up[None] * real_mode[:, None] + imag_up[None] * imag_mode[:, None]
    grad_imag = imag_up[None] * real_mode[:, None] - real_up[None] * imag_mode[:, None]
    real_low = upstream_modes[:, 0]
    imag_low = upstream_modes[:, 1]
    back_real = jnp.einsum(
        "iokm,okm->ikm", real_weight, real_low, preferred_element_type=jnp.float32
    ) + jnp.einsum("iokm,okm->ikm", imag_weight, imag_low, preferred_element_type=jnp.float32)
    back_imag = jnp.einsum(
        "iokm,okm->ikm", real_weight, imag_low, preferred_element_type=jnp.float32
    ) - jnp.einsum("iokm,okm->ikm", imag_weight, real_low, preferred_element_type=jnp.float32)
    return (jnp.stack([grad_real, grad_imag], axis=0), jnp.stack([back_real, back_imag], axis=1))


def gelu_slope(values):
    return (
        0.5 * (1.0 + lax.erf(values * 0.7071067811865476))
        + values * jnp.exp(-0.5 * values * values) * 0.3989422804014327
    )


def local(field, cotangent, spectral_weight, local_weight, bias):
    channels, width_x, width_y, depth_cells = field.shape
    kept_plane = MS * MT
    plane_table = plane_tables(NZ, NT, MS, MT)
    local_rows = lax.axis_index("gy") * width_y + jnp.arange(width_y, dtype=jnp.int32)
    cos_local, sin_local = axis_tables(NY, MS, local_rows)
    cos_across, sin_across = axis_tables(NX, MS, jnp.arange(NX, dtype=jnp.int32))

    def forward_chain(planes):
        coeffs = jnp.dot(
            planes.reshape(-1, depth_cells), plane_table, preferred_element_type=jnp.float32
        )
        coeffs = coeffs.astype(jnp.bfloat16).reshape(channels * width_x, width_y, 2, kept_plane)
        partial_terms = forward_axis(coeffs, cos_local, sin_local).astype(jnp.bfloat16)
        groups = lax.axis_size("gy")
        lead, parts, kept_rows, plane = partial_terms.shape
        pieces = partial_terms.reshape(lead, parts, groups, kept_rows // groups, plane)
        pieces = lax.all_to_all(pieces, "gy", split_axis=2, concat_axis=2, tiled=True)
        row_modes = jnp.sum(pieces.astype(jnp.float32), axis=2).astype(jnp.bfloat16)
        row_modes = row_modes.reshape(channels, width_x, 2, -1)
        blocks = lax.all_to_all(row_modes, "gx", split_axis=3, concat_axis=1, tiled=True)
        return forward_axis(blocks, cos_across, sin_across).astype(jnp.bfloat16)

    def inverse_chain(mode_values):
        across = inverse_axis(mode_values, cos_across, sin_across).astype(jnp.bfloat16)
        row_modes = lax.all_to_all(across, "gx", split_axis=1, concat_axis=3, tiled=True)
        row_modes = row_modes.reshape(channels * width_x, 2, -1, kept_plane)
        all_rows = lax.all_gather(row_modes, "gy", axis=2, tiled=True)
        cell_modes = inverse_axis(all_rows, cos_local, sin_local).astype(jnp.bfloat16)
        flattened = cell_modes.reshape(-1, 2 * kept_plane)
        summed = lax.dot_general(
            flattened, plane_table, (((1,), (1,)), ((), ())), preferred_element_type=jnp.float32
        )
        return summed.reshape(field.shape)

    field_modes = forward_chain(field)
    mixed_modes = spectral_apply(spectral_weight, field_modes)
    spectral = inverse_chain(mixed_modes)
    direct = jnp.einsum("io,ixyp->oxyp", local_weight, field, preferred_element_type=jnp.float32)
    before = spectral + direct + bias[:, None, None, None]
    upstream = (cotangent.astype(jnp.float32) * gelu_slope(before)).astype(jnp.bfloat16)
    upstream_modes = forward_chain(upstream)
    grad_weight, back_modes = spectral_adjoint(spectral_weight, field_modes, upstream_modes)
    returned = inverse_chain(back_modes.astype(jnp.bfloat16))
    direct_back = jnp.einsum(
        "io,oxyp->ixyp", local_weight, upstream, preferred_element_type=jnp.float32
    )
    return ((returned + direct_back).astype(jnp.bfloat16), grad_weight)


def solution(mesh):
    in_specs = (
        P(None, "gx", "gy", None),
        P(None, "gx", "gy", None),
        P(None, None, None, None, ("gy", "gx")),
        P(),
        P(),
    )
    out_specs = (P(None, "gx", "gy", None), P(None, None, None, None, ("gy", "gx")))
    return jax.shard_map(local, mesh=mesh, in_specs=in_specs, out_specs=out_specs, check_vma=False)
```

```python
import math

import jax
import jax.numpy as jnp
from jax import lax
from jax.sharding import PartitionSpec as P

NX = 128
NY = 128
NZ = 128
NT = 8
MS = 24
MT = 8


def axis_tables(length, kept_count, positions):
    half_kept = kept_count // 2
    mode_index = jnp.arange(kept_count, dtype=jnp.int32)
    frequency = jnp.where(mode_index < half_kept, mode_index, mode_index - kept_count)
    phases = jnp.mod(frequency[:, None] * positions[None, :], length)
    angles = phases.astype(jnp.float32) * (2.0 * math.pi / length)
    factor = 1.0 / math.sqrt(length)
    return (
        (jnp.cos(angles) * factor).astype(jnp.bfloat16),
        (jnp.sin(angles) * factor).astype(jnp.bfloat16),
    )


def plane_tables(depth_cells, time_steps, kept_count, kept_time):
    period = depth_cells * time_steps
    kept_plane = kept_count * kept_time
    depth_cos, depth_sin = unit_circle(depth_cells, kept_count, depth_cells, True)
    time_cos, time_sin = unit_circle(time_steps, kept_time, time_steps, False)

    def spread(depth_part, time_part):
        depth_wide = jnp.broadcast_to(
            depth_part[:, :, None], (depth_cells, kept_count, kept_time)
        ).reshape(depth_cells, 1, kept_plane)
        time_wide = jnp.broadcast_to(
            time_part[:, None, :], (time_steps, kept_count, kept_time)
        ).reshape(1, time_steps, kept_plane)
        return depth_wide, time_wide

    zc, tc = spread(depth_cos, time_cos)
    zs, ts = spread(depth_sin, time_sin)
    factor = 1.0 / math.sqrt(period)
    cos_sum = (zc * tc - zs * ts) * factor
    sin_sum = (zs * tc + zc * ts) * (-factor)
    table = jnp.concatenate([cos_sum, sin_sum], axis=2)
    return table.reshape(period, 2 * kept_plane).astype(jnp.bfloat16)


def unit_circle(length, kept_count, cells, centred):
    mode_index = jnp.arange(kept_count, dtype=jnp.int32)
    if centred:
        frequency = jnp.where(mode_index < kept_count // 2, mode_index, mode_index - kept_count)
    else:
        frequency = mode_index
    positions = jnp.arange(cells, dtype=jnp.int32)
    phases = jnp.mod(positions[:, None] * frequency[None, :], length)
    angles = phases.astype(jnp.float32) * (2.0 * math.pi / length)
    return jnp.cos(angles), jnp.sin(angles)


def forward_axis(values, cos_table, sin_table):
    with_cos = jnp.einsum("kn,lnrm->lrkm", cos_table, values, preferred_element_type=jnp.float32)
    with_sin = jnp.einsum("kn,lnrm->lrkm", sin_table, values, preferred_element_type=jnp.float32)
    real_part = with_cos[:, 0] + with_sin[:, 1]
    imag_part = with_cos[:, 1] - with_sin[:, 0]
    return jnp.stack([real_part, imag_part], axis=1)


def inverse_axis(values, cos_table, sin_table):
    with_cos = jnp.einsum("kn,lrkm->lnrm", cos_table, values, preferred_element_type=jnp.float32)
    with_sin = jnp.einsum("kn,lrkm->lnrm", sin_table, values, preferred_element_type=jnp.float32)
    real_part = with_cos[:, :, 0] - with_sin[:, :, 1]
    imag_part = with_cos[:, :, 1] + with_sin[:, :, 0]
    return jnp.stack([real_part, imag_part], axis=2)


def spectral_apply(weights, mode_values):
    real_weight, imag_weight = (weights[0], weights[1])
    real_mode, imag_mode = (mode_values[:, 0], mode_values[:, 1])
    out_real = jnp.einsum(
        "iokm,ikm->okm", real_weight, real_mode, preferred_element_type=jnp.float32
    ) - jnp.einsum("iokm,ikm->okm", imag_weight, imag_mode, preferred_element_type=jnp.float32)
    out_imag = jnp.einsum(
        "iokm,ikm->okm", real_weight, imag_mode, preferred_element_type=jnp.float32
    ) + jnp.einsum("iokm,ikm->okm", imag_weight, real_mode, preferred_element_type=jnp.float32)
    return jnp.stack([out_real, out_imag], axis=1).astype(jnp.bfloat16)


def spectral_adjoint(weights, mode_values, upstream_modes):
    real_weight, imag_weight = (weights[0], weights[1])
    real_mode = mode_values[:, 0].astype(jnp.float32)
    imag_mode = mode_values[:, 1].astype(jnp.float32)
    real_up = upstream_modes[:, 0].astype(jnp.float32)
    imag_up = upstream_modes[:, 1].astype(jnp.float32)
    grad_real = real_up[None] * real_mode[:, None] + imag_up[None] * imag_mode[:, None]
    grad_imag = imag_up[None] * real_mode[:, None] - real_up[None] * imag_mode[:, None]
    real_low = upstream_modes[:, 0]
    imag_low = upstream_modes[:, 1]
    back_real = jnp.einsum(
        "iokm,okm->ikm", real_weight, real_low, preferred_element_type=jnp.float32
    ) + jnp.einsum("iokm,okm->ikm", imag_weight, imag_low, preferred_element_type=jnp.float32)
    back_imag = jnp.einsum(
        "iokm,okm->ikm", real_weight, imag_low, preferred_element_type=jnp.float32
    ) - jnp.einsum("iokm,okm->ikm", imag_weight, real_low, preferred_element_type=jnp.float32)
    return (jnp.stack([grad_real, grad_imag], axis=0), jnp.stack([back_real, back_imag], axis=1))


def gelu_slope(values):
    return (
        0.5 * (1.0 + lax.erf(values * 0.7071067811865476))
        + values * jnp.exp(-0.5 * values * values) * 0.3989422804014327
    )


def local(field, cotangent, spectral_weight, local_weight, bias):
    channels, width_x, width_y, depth_cells = field.shape
    kept_plane = MS * MT
    plane_table = plane_tables(NZ, NT, MS, MT)
    local_rows = lax.axis_index("gy") * width_y + jnp.arange(width_y, dtype=jnp.int32)
    cos_local, sin_local = axis_tables(NY, MS, local_rows)
    cos_across, sin_across = axis_tables(NX, MS, jnp.arange(NX, dtype=jnp.int32))

    def forward_chain(planes):
        coeffs = jnp.dot(
            planes.reshape(-1, depth_cells), plane_table, preferred_element_type=jnp.float32
        )
        coeffs = coeffs.astype(jnp.bfloat16).reshape(channels * width_x, width_y, 2, kept_plane)
        partial_terms = forward_axis(coeffs, cos_local, sin_local).astype(jnp.bfloat16)
        groups = lax.axis_size("gy")
        lead, parts, kept_rows, plane = partial_terms.shape
        pieces = partial_terms.reshape(lead, parts, groups, kept_rows // groups, plane)
        pieces = lax.all_to_all(pieces, "gy", split_axis=2, concat_axis=2, tiled=True)
        row_modes = jnp.sum(pieces.astype(jnp.float32), axis=2).astype(jnp.bfloat16)
        row_modes = row_modes.reshape(channels, width_x, 2, -1)
        blocks = lax.all_to_all(row_modes, "gx", split_axis=3, concat_axis=1, tiled=True)
        return forward_axis(blocks, cos_across, sin_across).astype(jnp.bfloat16)

    def inverse_chain(mode_values):
        across = inverse_axis(mode_values, cos_across, sin_across).astype(jnp.bfloat16)
        row_modes = lax.all_to_all(across, "gx", split_axis=1, concat_axis=3, tiled=True)
        row_modes = row_modes.reshape(channels * width_x, 2, -1, kept_plane)
        all_rows = lax.all_gather(row_modes, "gy", axis=2, tiled=True)
        cell_modes = inverse_axis(all_rows, cos_local, sin_local).astype(jnp.bfloat16)
        flattened = cell_modes.reshape(-1, 2 * kept_plane)
        summed = lax.dot_general(
            flattened, plane_table, (((1,), (1,)), ((), ())), preferred_element_type=jnp.float32
        )
        return summed.reshape(field.shape)

    field_modes = forward_chain(field)
    mixed_modes = spectral_apply(spectral_weight, field_modes)
    spectral = inverse_chain(mixed_modes)
    direct = jnp.einsum("io,ixyp->oxyp", local_weight, field, preferred_element_type=jnp.float32)
    before = spectral + direct + bias[:, None, None, None]
    upstream = (cotangent.astype(jnp.float32) * gelu_slope(before)).astype(jnp.bfloat16)
    upstream_modes = forward_chain(upstream)
    grad_weight, back_modes = spectral_adjoint(spectral_weight, field_modes, upstream_modes)
    returned = inverse_chain(back_modes.astype(jnp.bfloat16))
    direct_back = jnp.einsum(
        "io,oxyp->ixyp", local_weight, upstream, preferred_element_type=jnp.float32
    )
    return ((returned + direct_back).astype(jnp.bfloat16), grad_weight)


def solution(mesh):
    in_specs = (
        P(None, "gx", "gy", None),
        P(None, "gx", "gy", None),
        P(None, None, None, None, ("gy", "gx")),
        P(),
        P(),
    )
    out_specs = (P(None, "gx", "gy", None), P(None, None, None, None, ("gy", "gx")))
    return jax.shard_map(local, mesh=mesh, in_specs=in_specs, out_specs=out_specs, check_vma=False)
```

```python
import math

import jax
import jax.numpy as jnp
from jax import lax
from jax.sharding import PartitionSpec as P

NX = 128
NY = 128
NZ = 128
NT = 8
MS = 24
MT = 8


def axis_tables(length, kept_count, positions):
    half_kept = kept_count // 2
    mode_index = jnp.arange(kept_count, dtype=jnp.int32)
    frequency = jnp.where(mode_index < half_kept, mode_index, mode_index - kept_count)
    phases = jnp.mod(frequency[:, None] * positions[None, :], length)
    angles = phases.astype(jnp.float32) * (2.0 * math.pi / length)
    factor = 1.0 / math.sqrt(length)
    return (
        (jnp.cos(angles) * factor).astype(jnp.bfloat16),
        (jnp.sin(angles) * factor).astype(jnp.bfloat16),
    )


def plane_tables(depth_cells, time_steps, kept_count, kept_time):
    period = depth_cells * time_steps
    kept_plane = kept_count * kept_time
    depth_cos, depth_sin = unit_circle(depth_cells, kept_count, depth_cells, True)
    time_cos, time_sin = unit_circle(time_steps, kept_time, time_steps, False)

    def spread(depth_part, time_part):
        depth_wide = jnp.broadcast_to(
            depth_part[:, :, None], (depth_cells, kept_count, kept_time)
        ).reshape(depth_cells, 1, kept_plane)
        time_wide = jnp.broadcast_to(
            time_part[:, None, :], (time_steps, kept_count, kept_time)
        ).reshape(1, time_steps, kept_plane)
        return depth_wide, time_wide

    zc, tc = spread(depth_cos, time_cos)
    zs, ts = spread(depth_sin, time_sin)
    factor = 1.0 / math.sqrt(period)
    cos_sum = (zc * tc - zs * ts) * factor
    sin_sum = (zs * tc + zc * ts) * (-factor)
    table = jnp.concatenate([cos_sum, sin_sum], axis=2)
    return table.reshape(period, 2 * kept_plane).astype(jnp.bfloat16)


def unit_circle(length, kept_count, cells, centred):
    mode_index = jnp.arange(kept_count, dtype=jnp.int32)
    if centred:
        frequency = jnp.where(mode_index < kept_count // 2, mode_index, mode_index - kept_count)
    else:
        frequency = mode_index
    positions = jnp.arange(cells, dtype=jnp.int32)
    phases = jnp.mod(positions[:, None] * frequency[None, :], length)
    angles = phases.astype(jnp.float32) * (2.0 * math.pi / length)
    return jnp.cos(angles), jnp.sin(angles)


def forward_axis(values, cos_table, sin_table):
    with_cos = jnp.einsum("kn,lnrm->lrkm", cos_table, values, preferred_element_type=jnp.float32)
    with_sin = jnp.einsum("kn,lnrm->lrkm", sin_table, values, preferred_element_type=jnp.float32)
    real_part = with_cos[:, 0] + with_sin[:, 1]
    imag_part = with_cos[:, 1] - with_sin[:, 0]
    return jnp.stack([real_part, imag_part], axis=1)


def inverse_axis(values, cos_table, sin_table):
    with_cos = jnp.einsum("kn,lrkm->lnrm", cos_table, values, preferred_element_type=jnp.float32)
    with_sin = jnp.einsum("kn,lrkm->lnrm", sin_table, values, preferred_element_type=jnp.float32)
    real_part = with_cos[:, :, 0] - with_sin[:, :, 1]
    imag_part = with_cos[:, :, 1] + with_sin[:, :, 0]
    return jnp.stack([real_part, imag_part], axis=2)


def spectral_apply(weights, mode_values):
    real_weight, imag_weight = (weights[0], weights[1])
    real_mode, imag_mode = (mode_values[:, 0], mode_values[:, 1])
    out_real = jnp.einsum(
        "iokm,ikm->okm", real_weight, real_mode, preferred_element_type=jnp.float32
    ) - jnp.einsum("iokm,ikm->okm", imag_weight, imag_mode, preferred_element_type=jnp.float32)
    out_imag = jnp.einsum(
        "iokm,ikm->okm", real_weight, imag_mode, preferred_element_type=jnp.float32
    ) + jnp.einsum("iokm,ikm->okm", imag_weight, real_mode, preferred_element_type=jnp.float32)
    return jnp.stack([out_real, out_imag], axis=1).astype(jnp.bfloat16)


def spectral_adjoint(weights, mode_values, upstream_modes):
    real_weight, imag_weight = (weights[0], weights[1])
    real_mode = mode_values[:, 0].astype(jnp.float32)
    imag_mode = mode_values[:, 1].astype(jnp.float32)
    real_up = upstream_modes[:, 0].astype(jnp.float32)
    imag_up = upstream_modes[:, 1].astype(jnp.float32)
    grad_real = real_up[None] * real_mode[:, None] + imag_up[None] * imag_mode[:, None]
    grad_imag = imag_up[None] * real_mode[:, None] - real_up[None] * imag_mode[:, None]
    real_low = upstream_modes[:, 0]
    imag_low = upstream_modes[:, 1]
    back_real = jnp.einsum(
        "iokm,okm->ikm", real_weight, real_low, preferred_element_type=jnp.float32
    ) + jnp.einsum("iokm,okm->ikm", imag_weight, imag_low, preferred_element_type=jnp.float32)
    back_imag = jnp.einsum(
        "iokm,okm->ikm", real_weight, imag_low, preferred_element_type=jnp.float32
    ) - jnp.einsum("iokm,okm->ikm", imag_weight, real_low, preferred_element_type=jnp.float32)
    return (jnp.stack([grad_real, grad_imag], axis=0), jnp.stack([back_real, back_imag], axis=1))


def gelu_slope(values):
    return (
        0.5 * (1.0 + lax.erf(values * 0.7071067811865476))
        + values * jnp.exp(-0.5 * values * values) * 0.3989422804014327
    )


def local(field, cotangent, spectral_weight, local_weight, bias):
    channels, width_x, width_y, depth_cells = field.shape
    kept_plane = MS * MT
    plane_table = plane_tables(NZ, NT, MS, MT)
    local_rows = lax.axis_index("gy") * width_y + jnp.arange(width_y, dtype=jnp.int32)
    cos_local, sin_local = axis_tables(NY, MS, local_rows)
    cos_across, sin_across = axis_tables(NX, MS, jnp.arange(NX, dtype=jnp.int32))

    plane_cos = plane_table[:, :kept_plane]
    plane_sin = plane_table[:, kept_plane:]
    forward_real = jnp.stack([cos_local, -sin_local], axis=0)
    forward_imag = jnp.stack([sin_local, cos_local], axis=0)

    def forward_chain(planes):
        flat = planes.reshape(-1, depth_cells)
        lead = channels * width_x

        def plane_part(table):
            part = jnp.dot(flat, table, preferred_element_type=jnp.float32)
            return part.astype(jnp.bfloat16).reshape(lead, width_y, kept_plane)

        real, imag = plane_part(plane_cos), plane_part(plane_sin)
        partial_terms = jnp.einsum(
            "pkn,lnm->lpkm", forward_real, real, preferred_element_type=jnp.float32
        ) + jnp.einsum("pkn,lnm->lpkm", forward_imag, imag, preferred_element_type=jnp.float32)
        partial_terms = partial_terms.astype(jnp.bfloat16)
        groups = lax.axis_size("gy")
        lead, parts, kept_rows, plane = partial_terms.shape
        pieces = partial_terms.reshape(lead, parts, groups, kept_rows // groups, plane)
        pieces = lax.all_to_all(pieces, "gy", split_axis=2, concat_axis=2, tiled=True)
        row_modes = jnp.sum(pieces.astype(jnp.float32), axis=2).astype(jnp.bfloat16)
        row_modes = row_modes.reshape(channels, width_x, 2, -1)
        blocks = lax.all_to_all(row_modes, "gx", split_axis=3, concat_axis=1, tiled=True)
        return forward_axis(blocks, cos_across, sin_across).astype(jnp.bfloat16)

    def inverse_chain(mode_values):
        across = inverse_axis(mode_values, cos_across, sin_across).astype(jnp.bfloat16)
        row_modes = lax.all_to_all(across, "gx", split_axis=1, concat_axis=3, tiled=True)
        row_modes = row_modes.reshape(channels * width_x, 2, -1, kept_plane)
        all_rows = lax.all_gather(row_modes, "gy", axis=2, tiled=True)
        summed = 0.0
        for rows_table, table in ((forward_real, plane_cos), (forward_imag, plane_sin)):
            part = jnp.einsum("pkn,lpkm->lnm", rows_table, all_rows, preferred_element_type=jnp.float32)
            part = part.astype(jnp.bfloat16).reshape(-1, kept_plane)
            summed = summed + lax.dot_general(
                part, table, (((1,), (1,)), ((), ())), preferred_element_type=jnp.float32
            )
        return summed.reshape(field.shape)

    field_modes = forward_chain(field)
    mixed_modes = spectral_apply(spectral_weight, field_modes)
    spectral = inverse_chain(mixed_modes)
    direct = jnp.einsum("io,ixyp->oxyp", local_weight, field, preferred_element_type=jnp.float32)
    before = spectral + direct + bias[:, None, None, None]
    upstream = (cotangent.astype(jnp.float32) * gelu_slope(before)).astype(jnp.bfloat16)
    upstream_modes = forward_chain(upstream)
    grad_weight, back_modes = spectral_adjoint(spectral_weight, field_modes, upstream_modes)
    returned = inverse_chain(back_modes.astype(jnp.bfloat16))
    direct_back = jnp.einsum(
        "io,oxyp->ixyp", local_weight, upstream, preferred_element_type=jnp.float32
    )
    return ((returned + direct_back).astype(jnp.bfloat16), grad_weight)


def solution(mesh):
    in_specs = (
        P(None, "gx", "gy", None),
        P(None, "gx", "gy", None),
        P(None, None, None, None, ("gy", "gx")),
        P(),
        P(),
    )
    out_specs = (P(None, "gx", "gy", None), P(None, None, None, None, ("gy", "gx")))
    return jax.shard_map(local, mesh=mesh, in_specs=in_specs, out_specs=out_specs, check_vma=False)
```

```python
import math

import jax
import jax.numpy as jnp
from jax import lax
from jax.sharding import PartitionSpec as P

NX = 128
NY = 128
NZ = 128
NT = 8
MS = 24
MT = 8


def axis_tables(length, kept_count, positions):
    half_kept = kept_count // 2
    mode_index = jnp.arange(kept_count, dtype=jnp.int32)
    frequency = jnp.where(mode_index < half_kept, mode_index, mode_index - kept_count)
    phases = jnp.mod(frequency[:, None] * positions[None, :], length)
    angles = phases.astype(jnp.float32) * (2.0 * math.pi / length)
    factor = 1.0 / math.sqrt(length)
    return (
        (jnp.cos(angles) * factor).astype(jnp.bfloat16),
        (jnp.sin(angles) * factor).astype(jnp.bfloat16),
    )


def plane_tables(depth_cells, time_steps, kept_count, kept_time):
    period = depth_cells * time_steps
    kept_plane = kept_count * kept_time
    depth_cos, depth_sin = unit_circle(depth_cells, kept_count, depth_cells, True)
    time_cos, time_sin = unit_circle(time_steps, kept_time, time_steps, False)

    def spread(depth_part, time_part):
        depth_wide = jnp.broadcast_to(
            depth_part[:, :, None], (depth_cells, kept_count, kept_time)
        ).reshape(depth_cells, 1, kept_plane)
        time_wide = jnp.broadcast_to(
            time_part[:, None, :], (time_steps, kept_count, kept_time)
        ).reshape(1, time_steps, kept_plane)
        return depth_wide, time_wide

    zc, tc = spread(depth_cos, time_cos)
    zs, ts = spread(depth_sin, time_sin)
    factor = 1.0 / math.sqrt(period)
    cos_sum = (zc * tc - zs * ts) * factor
    sin_sum = (zs * tc + zc * ts) * (-factor)
    table = jnp.concatenate([cos_sum, sin_sum], axis=2)
    return table.reshape(period, 2 * kept_plane).astype(jnp.bfloat16)


def unit_circle(length, kept_count, cells, centred):
    mode_index = jnp.arange(kept_count, dtype=jnp.int32)
    if centred:
        frequency = jnp.where(mode_index < kept_count // 2, mode_index, mode_index - kept_count)
    else:
        frequency = mode_index
    positions = jnp.arange(cells, dtype=jnp.int32)
    phases = jnp.mod(positions[:, None] * frequency[None, :], length)
    angles = phases.astype(jnp.float32) * (2.0 * math.pi / length)
    return jnp.cos(angles), jnp.sin(angles)


def forward_axis(values, cos_table, sin_table):
    with_cos = jnp.einsum("kn,lnrm->lrkm", cos_table, values, preferred_element_type=jnp.float32)
    with_sin = jnp.einsum("kn,lnrm->lrkm", sin_table, values, preferred_element_type=jnp.float32)
    real_part = with_cos[:, 0] + with_sin[:, 1]
    imag_part = with_cos[:, 1] - with_sin[:, 0]
    return jnp.stack([real_part, imag_part], axis=1)


def inverse_axis(values, cos_table, sin_table):
    with_cos = jnp.einsum("kn,lrkm->lnrm", cos_table, values, preferred_element_type=jnp.float32)
    with_sin = jnp.einsum("kn,lrkm->lnrm", sin_table, values, preferred_element_type=jnp.float32)
    real_part = with_cos[:, :, 0] - with_sin[:, :, 1]
    imag_part = with_cos[:, :, 1] + with_sin[:, :, 0]
    return jnp.stack([real_part, imag_part], axis=2)


def spectral_apply(weights, mode_values):
    real_weight, imag_weight = (weights[0], weights[1])
    real_mode, imag_mode = (mode_values[:, 0], mode_values[:, 1])
    out_real = jnp.einsum(
        "iokm,ikm->okm", real_weight, real_mode, preferred_element_type=jnp.float32
    ) - jnp.einsum("iokm,ikm->okm", imag_weight, imag_mode, preferred_element_type=jnp.float32)
    out_imag = jnp.einsum(
        "iokm,ikm->okm", real_weight, imag_mode, preferred_element_type=jnp.float32
    ) + jnp.einsum("iokm,ikm->okm", imag_weight, real_mode, preferred_element_type=jnp.float32)
    return jnp.stack([out_real, out_imag], axis=1).astype(jnp.bfloat16)


def spectral_adjoint(weights, mode_values, upstream_modes):
    real_weight, imag_weight = (weights[0], weights[1])
    real_mode = mode_values[:, 0].astype(jnp.float32)
    imag_mode = mode_values[:, 1].astype(jnp.float32)
    real_up = upstream_modes[:, 0].astype(jnp.float32)
    imag_up = upstream_modes[:, 1].astype(jnp.float32)
    grad_real = real_up[None] * real_mode[:, None] + imag_up[None] * imag_mode[:, None]
    grad_imag = imag_up[None] * real_mode[:, None] - real_up[None] * imag_mode[:, None]
    real_low = upstream_modes[:, 0]
    imag_low = upstream_modes[:, 1]
    back_real = jnp.einsum(
        "iokm,okm->ikm", real_weight, real_low, preferred_element_type=jnp.float32
    ) + jnp.einsum("iokm,okm->ikm", imag_weight, imag_low, preferred_element_type=jnp.float32)
    back_imag = jnp.einsum(
        "iokm,okm->ikm", real_weight, imag_low, preferred_element_type=jnp.float32
    ) - jnp.einsum("iokm,okm->ikm", imag_weight, real_low, preferred_element_type=jnp.float32)
    return (jnp.stack([grad_real, grad_imag], axis=0), jnp.stack([back_real, back_imag], axis=1))


def spectral_apply_blocks(weights, mode_values):
    real_weight, imag_weight = (weights[0], weights[1])
    real_mode, imag_mode = (mode_values[:, 0], mode_values[:, 1])

    def mix(w, v):
        return jnp.einsum("iokm,kim->kom", w, v, preferred_element_type=jnp.float32)

    out_real = mix(real_weight, real_mode) - mix(imag_weight, imag_mode)
    out_imag = mix(real_weight, imag_mode) + mix(imag_weight, real_mode)
    return jnp.stack([out_real, out_imag], axis=1).astype(jnp.bfloat16)


def spectral_adjoint_blocks(weights, mode_values, upstream_modes):
    real_weight, imag_weight = (weights[0], weights[1])
    real_mode = jnp.transpose(mode_values[:, 0], (1, 0, 2)).astype(jnp.float32)
    imag_mode = jnp.transpose(mode_values[:, 1], (1, 0, 2)).astype(jnp.float32)
    real_up = jnp.transpose(upstream_modes[:, 0], (1, 0, 2)).astype(jnp.float32)
    imag_up = jnp.transpose(upstream_modes[:, 1], (1, 0, 2)).astype(jnp.float32)
    grad_real = real_up[None] * real_mode[:, None] + imag_up[None] * imag_mode[:, None]
    grad_imag = imag_up[None] * real_mode[:, None] - real_up[None] * imag_mode[:, None]
    real_low = upstream_modes[:, 0]
    imag_low = upstream_modes[:, 1]

    def mix(w, v):
        return jnp.einsum("iokm,kom->kim", w, v, preferred_element_type=jnp.float32)

    back_real = mix(real_weight, real_low) + mix(imag_weight, imag_low)
    back_imag = mix(real_weight, imag_low) - mix(imag_weight, real_low)
    return (jnp.stack([grad_real, grad_imag], axis=0), jnp.stack([back_real, back_imag], axis=1))


def gelu_slope(values):
    return (
        0.5 * (1.0 + lax.erf(values * 0.7071067811865476))
        + values * jnp.exp(-0.5 * values * values) * 0.3989422804014327
    )


def local(field, cotangent, spectral_weight, local_weight, bias):
    channels, width_x, width_y, depth_cells = field.shape
    kept_plane = MS * MT
    plane_table = plane_tables(NZ, NT, MS, MT)
    local_rows = lax.axis_index("gy") * width_y + jnp.arange(width_y, dtype=jnp.int32)
    cos_local, sin_local = axis_tables(NY, MS, local_rows)
    cos_across, sin_across = axis_tables(NX, MS, jnp.arange(NX, dtype=jnp.int32))

    plane_cos = plane_table[:, :kept_plane]
    plane_sin = plane_table[:, kept_plane:]
    forward_real = jnp.stack([cos_local, -sin_local], axis=0)
    forward_imag = jnp.stack([sin_local, cos_local], axis=0)

    sharers = lax.axis_size("gx")
    share = MS * kept_plane // lax.axis_size("gy") // sharers
    across_forward = jnp.stack(
        [jnp.stack([cos_across, sin_across], axis=2), jnp.stack([-sin_across, cos_across], axis=2)],
        axis=1,
    )
    across_inverse = jnp.stack(
        [jnp.stack([cos_across.T, -sin_across.T], axis=2), jnp.stack([sin_across.T, cos_across.T], axis=2)],
        axis=1,
    )

    def forward_chain(planes):
        flat = planes.reshape(-1, depth_cells)
        lead = channels * width_x

        def plane_part(table):
            part = jnp.dot(flat, table, preferred_element_type=jnp.float32)
            return part.astype(jnp.bfloat16).reshape(lead, width_y, kept_plane)

        real, imag = plane_part(plane_cos), plane_part(plane_sin)
        partial_terms = jnp.einsum(
            "pkn,lnm->lpkm", forward_real, real, preferred_element_type=jnp.float32
        ) + jnp.einsum("pkn,lnm->lpkm", forward_imag, imag, preferred_element_type=jnp.float32)
        partial_terms = partial_terms.astype(jnp.bfloat16)
        groups = lax.axis_size("gy")
        lead, parts, kept_rows, plane = partial_terms.shape
        pieces = partial_terms.reshape(lead, parts, groups, kept_rows // groups, plane)
        pieces = lax.all_to_all(pieces, "gy", split_axis=2, concat_axis=2, tiled=True)
        row_modes = jnp.sum(pieces.astype(jnp.float32), axis=2).astype(jnp.bfloat16)
        row_modes = row_modes.reshape(channels, width_x, 2, sharers, share)
        row_modes = jnp.transpose(row_modes, (3, 1, 2, 0, 4))
        blocks = lax.all_to_all(row_modes, "gx", split_axis=0, concat_axis=0, tiled=True)
        blocks = blocks.reshape(sharers * width_x, 2, channels * share)
        modes = jnp.einsum(
            "kpxr,xrq->kpq", across_forward, blocks, preferred_element_type=jnp.float32
        )
        return modes.astype(jnp.bfloat16).reshape(MS, 2, channels, share)

    def inverse_chain(mode_values):
        flat = mode_values.reshape(MS, 2, channels * share)
        across = jnp.einsum(
            "xrkp,kpq->xrq", across_inverse, flat, preferred_element_type=jnp.float32
        ).astype(jnp.bfloat16)
        across = across.reshape(sharers, width_x, 2, channels, share)
        row_modes = lax.all_to_all(across, "gx", split_axis=0, concat_axis=0, tiled=True)
        row_modes = jnp.transpose(row_modes, (3, 1, 2, 0, 4))
        row_modes = row_modes.reshape(channels * width_x, 2, -1, kept_plane)
        all_rows = lax.all_gather(row_modes, "gy", axis=2, tiled=True)
        summed = 0.0
        for rows_table, table in ((forward_real, plane_cos), (forward_imag, plane_sin)):
            part = jnp.einsum("pkn,lpkm->lnm", rows_table, all_rows, preferred_element_type=jnp.float32)
            part = part.astype(jnp.bfloat16).reshape(-1, kept_plane)
            summed = summed + lax.dot_general(
                part, table, (((1,), (1,)), ((), ())), preferred_element_type=jnp.float32
            )
        return summed.reshape(field.shape)

    field_modes = forward_chain(field)
    mixed_modes = spectral_apply_blocks(spectral_weight, field_modes)
    spectral = inverse_chain(mixed_modes)
    direct = jnp.einsum("io,ixyp->oxyp", local_weight, field, preferred_element_type=jnp.float32)
    before = spectral + direct + bias[:, None, None, None]
    upstream = (cotangent.astype(jnp.float32) * gelu_slope(before)).astype(jnp.bfloat16)
    upstream_modes = forward_chain(upstream)
    grad_weight, back_modes = spectral_adjoint_blocks(spectral_weight, field_modes, upstream_modes)
    returned = inverse_chain(back_modes.astype(jnp.bfloat16))
    direct_back = jnp.einsum(
        "io,oxyp->ixyp", local_weight, upstream, preferred_element_type=jnp.float32
    )
    return ((returned + direct_back).astype(jnp.bfloat16), grad_weight)


def solution(mesh):
    in_specs = (
        P(None, "gx", "gy", None),
        P(None, "gx", "gy", None),
        P(None, None, None, None, ("gy", "gx")),
        P(),
        P(),
    )
    out_specs = (P(None, "gx", "gy", None), P(None, None, None, None, ("gy", "gx")))
    return jax.shard_map(local, mesh=mesh, in_specs=in_specs, out_specs=out_specs, check_vma=False)
```

```python
import math

import jax
import jax.numpy as jnp
from jax import lax
from jax.sharding import PartitionSpec as P

NX = 128
NY = 128
NZ = 128
NT = 8
MS = 24
MT = 8


def axis_tables(length, kept_count, positions):
    half_kept = kept_count // 2
    mode_index = jnp.arange(kept_count, dtype=jnp.int32)
    frequency = jnp.where(mode_index < half_kept, mode_index, mode_index - kept_count)
    phases = jnp.mod(frequency[:, None] * positions[None, :], length)
    angles = phases.astype(jnp.float32) * (2.0 * math.pi / length)
    factor = 1.0 / math.sqrt(length)
    return (
        (jnp.cos(angles) * factor).astype(jnp.bfloat16),
        (jnp.sin(angles) * factor).astype(jnp.bfloat16),
    )


def plane_tables(depth_cells, time_steps, kept_count, kept_time):
    period = depth_cells * time_steps
    kept_plane = kept_count * kept_time
    depth_cos, depth_sin = unit_circle(depth_cells, kept_count, depth_cells, True)
    time_cos, time_sin = unit_circle(time_steps, kept_time, time_steps, False)

    def spread(depth_part, time_part):
        depth_wide = jnp.broadcast_to(
            depth_part[:, :, None], (depth_cells, kept_count, kept_time)
        ).reshape(depth_cells, 1, kept_plane)
        time_wide = jnp.broadcast_to(
            time_part[:, None, :], (time_steps, kept_count, kept_time)
        ).reshape(1, time_steps, kept_plane)
        return depth_wide, time_wide

    zc, tc = spread(depth_cos, time_cos)
    zs, ts = spread(depth_sin, time_sin)
    factor = 1.0 / math.sqrt(period)
    cos_sum = (zc * tc - zs * ts) * factor
    sin_sum = (zs * tc + zc * ts) * (-factor)
    table = jnp.concatenate([cos_sum, sin_sum], axis=2)
    return table.reshape(period, 2 * kept_plane).astype(jnp.bfloat16)


def unit_circle(length, kept_count, cells, centred):
    mode_index = jnp.arange(kept_count, dtype=jnp.int32)
    if centred:
        frequency = jnp.where(mode_index < kept_count // 2, mode_index, mode_index - kept_count)
    else:
        frequency = mode_index
    positions = jnp.arange(cells, dtype=jnp.int32)
    phases = jnp.mod(positions[:, None] * frequency[None, :], length)
    angles = phases.astype(jnp.float32) * (2.0 * math.pi / length)
    return jnp.cos(angles), jnp.sin(angles)


def forward_axis(values, cos_table, sin_table):
    with_cos = jnp.einsum("kn,lnrm->lrkm", cos_table, values, preferred_element_type=jnp.float32)
    with_sin = jnp.einsum("kn,lnrm->lrkm", sin_table, values, preferred_element_type=jnp.float32)
    real_part = with_cos[:, 0] + with_sin[:, 1]
    imag_part = with_cos[:, 1] - with_sin[:, 0]
    return jnp.stack([real_part, imag_part], axis=1)


def inverse_axis(values, cos_table, sin_table):
    with_cos = jnp.einsum("kn,lrkm->lnrm", cos_table, values, preferred_element_type=jnp.float32)
    with_sin = jnp.einsum("kn,lrkm->lnrm", sin_table, values, preferred_element_type=jnp.float32)
    real_part = with_cos[:, :, 0] - with_sin[:, :, 1]
    imag_part = with_cos[:, :, 1] + with_sin[:, :, 0]
    return jnp.stack([real_part, imag_part], axis=2)


def spectral_apply(weights, mode_values):
    real_weight, imag_weight = (weights[0], weights[1])
    real_mode, imag_mode = (mode_values[:, 0], mode_values[:, 1])
    out_real = jnp.einsum(
        "iokm,ikm->okm", real_weight, real_mode, preferred_element_type=jnp.float32
    ) - jnp.einsum("iokm,ikm->okm", imag_weight, imag_mode, preferred_element_type=jnp.float32)
    out_imag = jnp.einsum(
        "iokm,ikm->okm", real_weight, imag_mode, preferred_element_type=jnp.float32
    ) + jnp.einsum("iokm,ikm->okm", imag_weight, real_mode, preferred_element_type=jnp.float32)
    return jnp.stack([out_real, out_imag], axis=1).astype(jnp.bfloat16)


def spectral_adjoint(weights, mode_values, upstream_modes):
    real_weight, imag_weight = (weights[0], weights[1])
    real_mode = mode_values[:, 0].astype(jnp.float32)
    imag_mode = mode_values[:, 1].astype(jnp.float32)
    real_up = upstream_modes[:, 0].astype(jnp.float32)
    imag_up = upstream_modes[:, 1].astype(jnp.float32)
    grad_real = real_up[None] * real_mode[:, None] + imag_up[None] * imag_mode[:, None]
    grad_imag = imag_up[None] * real_mode[:, None] - real_up[None] * imag_mode[:, None]
    real_low = upstream_modes[:, 0]
    imag_low = upstream_modes[:, 1]
    back_real = jnp.einsum(
        "iokm,okm->ikm", real_weight, real_low, preferred_element_type=jnp.float32
    ) + jnp.einsum("iokm,okm->ikm", imag_weight, imag_low, preferred_element_type=jnp.float32)
    back_imag = jnp.einsum(
        "iokm,okm->ikm", real_weight, imag_low, preferred_element_type=jnp.float32
    ) - jnp.einsum("iokm,okm->ikm", imag_weight, real_low, preferred_element_type=jnp.float32)
    return (jnp.stack([grad_real, grad_imag], axis=0), jnp.stack([back_real, back_imag], axis=1))


def gelu_slope(values):
    return (
        0.5 * (1.0 + lax.erf(values * 0.7071067811865476))
        + values * jnp.exp(-0.5 * values * values) * 0.3989422804014327
    )


def local(field, cotangent, spectral_weight, local_weight, bias):
    channels, width_x, width_y, depth_cells = field.shape
    kept_plane = MS * MT
    plane_table = plane_tables(NZ, NT, MS, MT)
    local_rows = lax.axis_index("gy") * width_y + jnp.arange(width_y, dtype=jnp.int32)
    cos_local, sin_local = axis_tables(NY, MS, local_rows)
    cos_across, sin_across = axis_tables(NX, MS, jnp.arange(NX, dtype=jnp.int32))

    plane_cos = plane_table[:, :kept_plane]
    plane_sin = plane_table[:, kept_plane:]
    forward_real = jnp.stack([cos_local, -sin_local], axis=0)
    forward_imag = jnp.stack([sin_local, cos_local], axis=0)

    groups = lax.axis_size("gy")
    row_group = lax.axis_index("gy")

    def forward_chain(planes):
        flat = planes.reshape(-1, depth_cells)
        lead = channels * width_x

        def plane_part(table):
            part = jnp.dot(flat, table, preferred_element_type=jnp.float32)
            return part.astype(jnp.bfloat16).reshape(lead, width_y, kept_plane)

        real, imag = plane_part(plane_cos), plane_part(plane_sin)
        partial_terms = jnp.einsum(
            "pkn,lnm->lpkm", forward_real, real, preferred_element_type=jnp.float32
        ) + jnp.einsum("pkn,lnm->lpkm", forward_imag, imag, preferred_element_type=jnp.float32)
        partial_terms = partial_terms.astype(jnp.bfloat16)
        lead, parts, kept_rows, plane = partial_terms.shape
        pieces = partial_terms.reshape(lead, parts, groups, kept_rows // groups, plane)
        total = lax.dynamic_index_in_dim(pieces, row_group, axis=2, keepdims=False)
        total = total.astype(jnp.float32)
        for shift in range(1, groups):
            sent = lax.dynamic_index_in_dim(pieces, (row_group + shift) % groups, axis=2, keepdims=False)
            got = lax.ppermute(sent, "gy", [(i, (i + shift) % groups) for i in range(groups)])
            total = total + got.astype(jnp.float32)
        row_modes = total.astype(jnp.bfloat16)
        row_modes = row_modes.reshape(channels, width_x, 2, -1)
        blocks = lax.all_to_all(row_modes, "gx", split_axis=3, concat_axis=1, tiled=True)
        return forward_axis(blocks, cos_across, sin_across).astype(jnp.bfloat16)

    def inverse_chain(mode_values):
        across = inverse_axis(mode_values, cos_across, sin_across).astype(jnp.bfloat16)
        row_modes = lax.all_to_all(across, "gx", split_axis=1, concat_axis=3, tiled=True)
        row_modes = row_modes.reshape(channels * width_x, 2, -1, kept_plane)
        block = row_modes.shape[2]
        cell_parts = [0.0, 0.0]
        for shift in range(groups):
            if shift:
                got = lax.ppermute(row_modes, "gy", [(i, (i + shift) % groups) for i in range(groups)])
            else:
                got = row_modes
            start = ((row_group - shift) % groups) * block
            for which, rows_table in enumerate((forward_real, forward_imag)):
                rows_part = lax.dynamic_slice_in_dim(rows_table, start, block, axis=1)
                cell_parts[which] = cell_parts[which] + jnp.einsum(
                    "pkn,lpkm->lnm", rows_part, got, preferred_element_type=jnp.float32
                )
        summed = 0.0
        for cell_part, table in zip(cell_parts, (plane_cos, plane_sin)):
            part = cell_part.astype(jnp.bfloat16).reshape(-1, kept_plane)
            summed = summed + lax.dot_general(
                part, table, (((1,), (1,)), ((), ())), preferred_element_type=jnp.float32
            )
        return summed.reshape(field.shape)

    field_modes = forward_chain(field)
    mixed_modes = spectral_apply(spectral_weight, field_modes)
    spectral = inverse_chain(mixed_modes)
    direct = jnp.einsum("io,ixyp->oxyp", local_weight, field, preferred_element_type=jnp.float32)
    before = spectral + direct + bias[:, None, None, None]
    upstream = (cotangent.astype(jnp.float32) * gelu_slope(before)).astype(jnp.bfloat16)
    upstream_modes = forward_chain(upstream)
    grad_weight, back_modes = spectral_adjoint(spectral_weight, field_modes, upstream_modes)
    returned = inverse_chain(back_modes.astype(jnp.bfloat16))
    direct_back = jnp.einsum(
        "io,oxyp->ixyp", local_weight, upstream, preferred_element_type=jnp.float32
    )
    return ((returned + direct_back).astype(jnp.bfloat16), grad_weight)


def solution(mesh):
    in_specs = (
        P(None, "gx", "gy", None),
        P(None, "gx", "gy", None),
        P(None, None, None, None, ("gy", "gx")),
        P(),
        P(),
    )
    out_specs = (P(None, "gx", "gy", None), P(None, None, None, None, ("gy", "gx")))
    return jax.shard_map(local, mesh=mesh, in_specs=in_specs, out_specs=out_specs, check_vma=False)
```

```python
import math

import jax
import jax.numpy as jnp
from jax import lax
from jax.sharding import PartitionSpec as P

NX = 128
NY = 128
NZ = 128
NT = 8
MS = 24
MT = 8


def axis_tables(length, kept_count, positions):
    half_kept = kept_count // 2
    mode_index = jnp.arange(kept_count, dtype=jnp.int32)
    frequency = jnp.where(mode_index < half_kept, mode_index, mode_index - kept_count)
    phases = jnp.mod(frequency[:, None] * positions[None, :], length)
    angles = phases.astype(jnp.float32) * (2.0 * math.pi / length)
    factor = 1.0 / math.sqrt(length)
    return (
        (jnp.cos(angles) * factor).astype(jnp.bfloat16),
        (jnp.sin(angles) * factor).astype(jnp.bfloat16),
    )


def plane_tables(depth_cells, time_steps, kept_count, kept_time):
    period = depth_cells * time_steps
    kept_plane = kept_count * kept_time
    depth_cos, depth_sin = unit_circle(depth_cells, kept_count, depth_cells, True)
    time_cos, time_sin = unit_circle(time_steps, kept_time, time_steps, False)

    def spread(depth_part, time_part):
        depth_wide = jnp.broadcast_to(
            depth_part[:, :, None], (depth_cells, kept_count, kept_time)
        ).reshape(depth_cells, 1, kept_plane)
        time_wide = jnp.broadcast_to(
            time_part[:, None, :], (time_steps, kept_count, kept_time)
        ).reshape(1, time_steps, kept_plane)
        return depth_wide, time_wide

    zc, tc = spread(depth_cos, time_cos)
    zs, ts = spread(depth_sin, time_sin)
    factor = 1.0 / math.sqrt(period)
    cos_sum = (zc * tc - zs * ts) * factor
    sin_sum = (zs * tc + zc * ts) * (-factor)
    table = jnp.concatenate([cos_sum, sin_sum], axis=2)
    return table.reshape(period, 2 * kept_plane).astype(jnp.bfloat16)


def unit_circle(length, kept_count, cells, centred):
    mode_index = jnp.arange(kept_count, dtype=jnp.int32)
    if centred:
        frequency = jnp.where(mode_index < kept_count // 2, mode_index, mode_index - kept_count)
    else:
        frequency = mode_index
    positions = jnp.arange(cells, dtype=jnp.int32)
    phases = jnp.mod(positions[:, None] * frequency[None, :], length)
    angles = phases.astype(jnp.float32) * (2.0 * math.pi / length)
    return jnp.cos(angles), jnp.sin(angles)


def forward_axis(values, cos_table, sin_table):
    with_cos = jnp.einsum("kn,lnrm->lrkm", cos_table, values, preferred_element_type=jnp.float32)
    with_sin = jnp.einsum("kn,lnrm->lrkm", sin_table, values, preferred_element_type=jnp.float32)
    real_part = with_cos[:, 0] + with_sin[:, 1]
    imag_part = with_cos[:, 1] - with_sin[:, 0]
    return jnp.stack([real_part, imag_part], axis=1)


def inverse_axis(values, cos_table, sin_table):
    with_cos = jnp.einsum("kn,lrkm->lnrm", cos_table, values, preferred_element_type=jnp.float32)
    with_sin = jnp.einsum("kn,lrkm->lnrm", sin_table, values, preferred_element_type=jnp.float32)
    real_part = with_cos[:, :, 0] - with_sin[:, :, 1]
    imag_part = with_cos[:, :, 1] + with_sin[:, :, 0]
    return jnp.stack([real_part, imag_part], axis=2)


def spectral_apply(weights, mode_values):
    real_mode, imag_mode = (mode_values[:, 0], mode_values[:, 1])
    arranged = jnp.stack(
        [jnp.stack([real_mode, imag_mode], axis=0), jnp.stack([-imag_mode, real_mode], axis=0)], axis=0
    )
    out = jnp.einsum("qiokm,qpikm->opkm", weights, arranged, preferred_element_type=jnp.float32)
    return out.astype(jnp.bfloat16)


def spectral_adjoint(weights, mode_values, upstream_modes):
    real_mode = mode_values[:, 0].astype(jnp.float32)
    imag_mode = mode_values[:, 1].astype(jnp.float32)
    real_up = upstream_modes[:, 0].astype(jnp.float32)
    imag_up = upstream_modes[:, 1].astype(jnp.float32)
    grad_real = real_up[None] * real_mode[:, None] + imag_up[None] * imag_mode[:, None]
    grad_imag = imag_up[None] * real_mode[:, None] - real_up[None] * imag_mode[:, None]
    real_low = upstream_modes[:, 0]
    imag_low = upstream_modes[:, 1]
    arranged = jnp.stack(
        [jnp.stack([real_low, imag_low], axis=0), jnp.stack([imag_low, -real_low], axis=0)], axis=0
    )
    back = jnp.einsum("qiokm,qpokm->ipkm", weights, arranged, preferred_element_type=jnp.float32)
    return (jnp.stack([grad_real, grad_imag], axis=0), back)


def gelu_slope(values):
    return (
        0.5 * (1.0 + lax.erf(values * 0.7071067811865476))
        + values * jnp.exp(-0.5 * values * values) * 0.3989422804014327
    )


def local(field, cotangent, spectral_weight, local_weight, bias):
    channels, width_x, width_y, depth_cells = field.shape
    kept_plane = MS * MT
    plane_table = plane_tables(NZ, NT, MS, MT)
    local_rows = lax.axis_index("gy") * width_y + jnp.arange(width_y, dtype=jnp.int32)
    cos_local, sin_local = axis_tables(NY, MS, local_rows)
    cos_across, sin_across = axis_tables(NX, MS, jnp.arange(NX, dtype=jnp.int32))

    plane_cos = plane_table[:, :kept_plane]
    plane_sin = plane_table[:, kept_plane:]
    forward_real = jnp.stack([cos_local, -sin_local], axis=0)
    forward_imag = jnp.stack([sin_local, cos_local], axis=0)

    def forward_chain(planes):
        flat = planes.reshape(-1, depth_cells)
        lead = channels * width_x

        def plane_part(table):
            part = jnp.dot(flat, table, preferred_element_type=jnp.float32)
            return part.astype(jnp.bfloat16).reshape(lead, width_y, kept_plane)

        real, imag = plane_part(plane_cos), plane_part(plane_sin)
        partial_terms = jnp.einsum(
            "pkn,lnm->lpkm", forward_real, real, preferred_element_type=jnp.float32
        ) + jnp.einsum("pkn,lnm->lpkm", forward_imag, imag, preferred_element_type=jnp.float32)
        partial_terms = partial_terms.astype(jnp.bfloat16)
        groups = lax.axis_size("gy")
        lead, parts, kept_rows, plane = partial_terms.shape
        pieces = partial_terms.reshape(lead, parts, groups, kept_rows // groups, plane)
        pieces = lax.all_to_all(pieces, "gy", split_axis=2, concat_axis=2, tiled=True)
        row_modes = jnp.sum(pieces.astype(jnp.float32), axis=2).astype(jnp.bfloat16)
        row_modes = row_modes.reshape(channels, width_x, 2, -1)
        blocks = lax.all_to_all(row_modes, "gx", split_axis=3, concat_axis=1, tiled=True)
        return forward_axis(blocks, cos_across, sin_across).astype(jnp.bfloat16)

    def inverse_chain(mode_values):
        across = inverse_axis(mode_values, cos_across, sin_across).astype(jnp.bfloat16)
        row_modes = lax.all_to_all(across, "gx", split_axis=1, concat_axis=3, tiled=True)
        row_modes = row_modes.reshape(channels * width_x, 2, -1, kept_plane)
        all_rows = lax.all_gather(row_modes, "gy", axis=2, tiled=True)
        summed = 0.0
        for rows_table, table in ((forward_real, plane_cos), (forward_imag, plane_sin)):
            part = jnp.einsum("pkn,lpkm->lnm", rows_table, all_rows, preferred_element_type=jnp.float32)
            part = part.astype(jnp.bfloat16).reshape(-1, kept_plane)
            summed = summed + lax.dot_general(
                part, table, (((1,), (1,)), ((), ())), preferred_element_type=jnp.float32
            )
        return summed.reshape(field.shape)

    field_modes = forward_chain(field)
    mixed_modes = spectral_apply(spectral_weight, field_modes)
    spectral = inverse_chain(mixed_modes)
    direct = jnp.einsum("io,ixyp->oxyp", local_weight, field, preferred_element_type=jnp.float32)
    before = spectral + direct + bias[:, None, None, None]
    upstream = (cotangent.astype(jnp.float32) * gelu_slope(before)).astype(jnp.bfloat16)
    upstream_modes = forward_chain(upstream)
    grad_weight, back_modes = spectral_adjoint(spectral_weight, field_modes, upstream_modes)
    returned = inverse_chain(back_modes.astype(jnp.bfloat16))
    direct_back = jnp.einsum(
        "io,oxyp->ixyp", local_weight, upstream, preferred_element_type=jnp.float32
    )
    return ((returned + direct_back).astype(jnp.bfloat16), grad_weight)


def solution(mesh):
    in_specs = (
        P(None, "gx", "gy", None),
        P(None, "gx", "gy", None),
        P(None, None, None, None, ("gy", "gx")),
        P(),
        P(),
    )
    out_specs = (P(None, "gx", "gy", None), P(None, None, None, None, ("gy", "gx")))
    return jax.shard_map(local, mesh=mesh, in_specs=in_specs, out_specs=out_specs, check_vma=False)
```

```python
import math

import jax
import jax.numpy as jnp
from jax import lax
from jax.sharding import PartitionSpec as P

NX = 128
NY = 128
NZ = 128
NT = 8
MS = 24
MT = 8


def axis_tables(length, kept_count, positions):
    half_kept = kept_count // 2
    mode_index = jnp.arange(kept_count, dtype=jnp.int32)
    frequency = jnp.where(mode_index < half_kept, mode_index, mode_index - kept_count)
    phases = jnp.mod(frequency[:, None] * positions[None, :], length)
    angles = phases.astype(jnp.float32) * (2.0 * math.pi / length)
    factor = 1.0 / math.sqrt(length)
    return (
        (jnp.cos(angles) * factor).astype(jnp.bfloat16),
        (jnp.sin(angles) * factor).astype(jnp.bfloat16),
    )


def plane_tables(depth_cells, time_steps, kept_count, kept_time):
    period = depth_cells * time_steps
    kept_plane = kept_count * kept_time
    depth_cos, depth_sin = unit_circle(depth_cells, kept_count, depth_cells, True)
    time_cos, time_sin = unit_circle(time_steps, kept_time, time_steps, False)

    def spread(depth_part, time_part):
        depth_wide = jnp.broadcast_to(
            depth_part[:, :, None], (depth_cells, kept_count, kept_time)
        ).reshape(depth_cells, 1, kept_plane)
        time_wide = jnp.broadcast_to(
            time_part[:, None, :], (time_steps, kept_count, kept_time)
        ).reshape(1, time_steps, kept_plane)
        return depth_wide, time_wide

    zc, tc = spread(depth_cos, time_cos)
    zs, ts = spread(depth_sin, time_sin)
    factor = 1.0 / math.sqrt(period)
    cos_sum = (zc * tc - zs * ts) * factor
    sin_sum = (zs * tc + zc * ts) * (-factor)
    table = jnp.concatenate([cos_sum, sin_sum], axis=2)
    return table.reshape(period, 2 * kept_plane).astype(jnp.bfloat16)


def unit_circle(length, kept_count, cells, centred):
    mode_index = jnp.arange(kept_count, dtype=jnp.int32)
    if centred:
        frequency = jnp.where(mode_index < kept_count // 2, mode_index, mode_index - kept_count)
    else:
        frequency = mode_index
    positions = jnp.arange(cells, dtype=jnp.int32)
    phases = jnp.mod(positions[:, None] * frequency[None, :], length)
    angles = phases.astype(jnp.float32) * (2.0 * math.pi / length)
    return jnp.cos(angles), jnp.sin(angles)


def forward_axis(values, cos_table, sin_table):
    with_cos = jnp.einsum("kn,lnrm->lrkm", cos_table, values, preferred_element_type=jnp.float32)
    with_sin = jnp.einsum("kn,lnrm->lrkm", sin_table, values, preferred_element_type=jnp.float32)
    real_part = with_cos[:, 0] + with_sin[:, 1]
    imag_part = with_cos[:, 1] - with_sin[:, 0]
    return jnp.stack([real_part, imag_part], axis=1)


def inverse_axis(values, cos_table, sin_table):
    with_cos = jnp.einsum("kn,lrkm->lnrm", cos_table, values, preferred_element_type=jnp.float32)
    with_sin = jnp.einsum("kn,lrkm->lnrm", sin_table, values, preferred_element_type=jnp.float32)
    real_part = with_cos[:, :, 0] - with_sin[:, :, 1]
    imag_part = with_cos[:, :, 1] + with_sin[:, :, 0]
    return jnp.stack([real_part, imag_part], axis=2)


def spectral_apply(weights, mode_values):
    real_weight = weights[0].astype(jnp.float32)
    imag_weight = weights[1].astype(jnp.float32)
    real_mode = mode_values[:, 0].astype(jnp.float32)[:, None]
    imag_mode = mode_values[:, 1].astype(jnp.float32)[:, None]
    out_real = jnp.sum(real_weight * real_mode - imag_weight * imag_mode, axis=0)
    out_imag = jnp.sum(real_weight * imag_mode + imag_weight * real_mode, axis=0)
    return jnp.stack([out_real, out_imag], axis=1).astype(jnp.bfloat16)


def spectral_adjoint(weights, mode_values, upstream_modes):
    real_weight = weights[0].astype(jnp.float32)
    imag_weight = weights[1].astype(jnp.float32)
    real_mode = mode_values[:, 0].astype(jnp.float32)
    imag_mode = mode_values[:, 1].astype(jnp.float32)
    real_up = upstream_modes[:, 0].astype(jnp.float32)
    imag_up = upstream_modes[:, 1].astype(jnp.float32)
    grad_real = real_up[None] * real_mode[:, None] + imag_up[None] * imag_mode[:, None]
    grad_imag = imag_up[None] * real_mode[:, None] - real_up[None] * imag_mode[:, None]
    back_real = jnp.sum(real_weight * real_up[None] + imag_weight * imag_up[None], axis=1)
    back_imag = jnp.sum(real_weight * imag_up[None] - imag_weight * real_up[None], axis=1)
    return (jnp.stack([grad_real, grad_imag], axis=0), jnp.stack([back_real, back_imag], axis=1))


def gelu_slope(values):
    return (
        0.5 * (1.0 + lax.erf(values * 0.7071067811865476))
        + values * jnp.exp(-0.5 * values * values) * 0.3989422804014327
    )


def local(field, cotangent, spectral_weight, local_weight, bias):
    channels, width_x, width_y, depth_cells = field.shape
    kept_plane = MS * MT
    plane_table = plane_tables(NZ, NT, MS, MT)
    local_rows = lax.axis_index("gy") * width_y + jnp.arange(width_y, dtype=jnp.int32)
    cos_local, sin_local = axis_tables(NY, MS, local_rows)
    cos_across, sin_across = axis_tables(NX, MS, jnp.arange(NX, dtype=jnp.int32))

    plane_cos = plane_table[:, :kept_plane]
    plane_sin = plane_table[:, kept_plane:]
    forward_real = jnp.stack([cos_local, -sin_local], axis=0)
    forward_imag = jnp.stack([sin_local, cos_local], axis=0)

    def forward_chain(planes):
        flat = planes.reshape(-1, depth_cells)
        lead = channels * width_x

        def plane_part(table):
            part = jnp.dot(flat, table, preferred_element_type=jnp.float32)
            return part.astype(jnp.bfloat16).reshape(lead, width_y, kept_plane)

        real, imag = plane_part(plane_cos), plane_part(plane_sin)
        partial_terms = jnp.einsum(
            "pkn,lnm->lpkm", forward_real, real, preferred_element_type=jnp.float32
        ) + jnp.einsum("pkn,lnm->lpkm", forward_imag, imag, preferred_element_type=jnp.float32)
        partial_terms = partial_terms.astype(jnp.bfloat16)
        groups = lax.axis_size("gy")
        lead, parts, kept_rows, plane = partial_terms.shape
        pieces = partial_terms.reshape(lead, parts, groups, kept_rows // groups, plane)
        pieces = lax.all_to_all(pieces, "gy", split_axis=2, concat_axis=2, tiled=True)
        row_modes = jnp.sum(pieces.astype(jnp.float32), axis=2).astype(jnp.bfloat16)
        row_modes = row_modes.reshape(channels, width_x, 2, -1)
        blocks = lax.all_to_all(row_modes, "gx", split_axis=3, concat_axis=1, tiled=True)
        return forward_axis(blocks, cos_across, sin_across).astype(jnp.bfloat16)

    def inverse_chain(mode_values):
        across = inverse_axis(mode_values, cos_across, sin_across).astype(jnp.bfloat16)
        row_modes = lax.all_to_all(across, "gx", split_axis=1, concat_axis=3, tiled=True)
        row_modes = row_modes.reshape(channels * width_x, 2, -1, kept_plane)
        all_rows = lax.all_gather(row_modes, "gy", axis=2, tiled=True)
        summed = 0.0
        for rows_table, table in ((forward_real, plane_cos), (forward_imag, plane_sin)):
            part = jnp.einsum("pkn,lpkm->lnm", rows_table, all_rows, preferred_element_type=jnp.float32)
            part = part.astype(jnp.bfloat16).reshape(-1, kept_plane)
            summed = summed + lax.dot_general(
                part, table, (((1,), (1,)), ((), ())), preferred_element_type=jnp.float32
            )
        return summed.reshape(field.shape)

    field_modes = forward_chain(field)
    mixed_modes = spectral_apply(spectral_weight, field_modes)
    spectral = inverse_chain(mixed_modes)
    direct = jnp.einsum("io,ixyp->oxyp", local_weight, field, preferred_element_type=jnp.float32)
    before = spectral + direct + bias[:, None, None, None]
    upstream = (cotangent.astype(jnp.float32) * gelu_slope(before)).astype(jnp.bfloat16)
    upstream_modes = forward_chain(upstream)
    grad_weight, back_modes = spectral_adjoint(spectral_weight, field_modes, upstream_modes)
    returned = inverse_chain(back_modes.astype(jnp.bfloat16))
    direct_back = jnp.einsum(
        "io,oxyp->ixyp", local_weight, upstream, preferred_element_type=jnp.float32
    )
    return ((returned + direct_back).astype(jnp.bfloat16), grad_weight)


def solution(mesh):
    in_specs = (
        P(None, "gx", "gy", None),
        P(None, "gx", "gy", None),
        P(None, None, None, None, ("gy", "gx")),
        P(),
        P(),
    )
    out_specs = (P(None, "gx", "gy", None), P(None, None, None, None, ("gy", "gx")))
    return jax.shard_map(local, mesh=mesh, in_specs=in_specs, out_specs=out_specs, check_vma=False)
```

```python
import math

import jax
import jax.numpy as jnp
from jax import lax
from jax.sharding import PartitionSpec as P

NX = 128
NY = 128
NZ = 128
NT = 8
MS = 24
MT = 8


def axis_tables(length, kept_count, positions):
    half_kept = kept_count // 2
    mode_index = jnp.arange(kept_count, dtype=jnp.int32)
    frequency = jnp.where(mode_index < half_kept, mode_index, mode_index - kept_count)
    phases = jnp.mod(frequency[:, None] * positions[None, :], length)
    angles = phases.astype(jnp.float32) * (2.0 * math.pi / length)
    factor = 1.0 / math.sqrt(length)
    return (
        (jnp.cos(angles) * factor).astype(jnp.bfloat16),
        (jnp.sin(angles) * factor).astype(jnp.bfloat16),
    )


def plane_tables(depth_cells, time_steps, kept_count, kept_time):
    period = depth_cells * time_steps
    kept_plane = kept_count * kept_time
    depth_cos, depth_sin = unit_circle(depth_cells, kept_count, depth_cells, True)
    time_cos, time_sin = unit_circle(time_steps, kept_time, time_steps, False)

    def spread(depth_part, time_part):
        depth_wide = jnp.broadcast_to(
            depth_part[:, :, None], (depth_cells, kept_count, kept_time)
        ).reshape(depth_cells, 1, kept_plane)
        time_wide = jnp.broadcast_to(
            time_part[:, None, :], (time_steps, kept_count, kept_time)
        ).reshape(1, time_steps, kept_plane)
        return depth_wide, time_wide

    zc, tc = spread(depth_cos, time_cos)
    zs, ts = spread(depth_sin, time_sin)
    factor = 1.0 / math.sqrt(period)
    cos_sum = (zc * tc - zs * ts) * factor
    sin_sum = (zs * tc + zc * ts) * (-factor)
    table = jnp.concatenate([cos_sum, sin_sum], axis=2)
    return table.reshape(period, 2 * kept_plane).astype(jnp.bfloat16)


def unit_circle(length, kept_count, cells, centred):
    mode_index = jnp.arange(kept_count, dtype=jnp.int32)
    if centred:
        frequency = jnp.where(mode_index < kept_count // 2, mode_index, mode_index - kept_count)
    else:
        frequency = mode_index
    positions = jnp.arange(cells, dtype=jnp.int32)
    phases = jnp.mod(positions[:, None] * frequency[None, :], length)
    angles = phases.astype(jnp.float32) * (2.0 * math.pi / length)
    return jnp.cos(angles), jnp.sin(angles)


def forward_axis(values, cos_table, sin_table):
    with_cos = jnp.einsum("kn,lnrm->lrkm", cos_table, values, preferred_element_type=jnp.float32)
    with_sin = jnp.einsum("kn,lnrm->lrkm", sin_table, values, preferred_element_type=jnp.float32)
    real_part = with_cos[:, 0] + with_sin[:, 1]
    imag_part = with_cos[:, 1] - with_sin[:, 0]
    return jnp.stack([real_part, imag_part], axis=1)


def inverse_axis(values, cos_table, sin_table):
    with_cos = jnp.einsum("kn,lrkm->lnrm", cos_table, values, preferred_element_type=jnp.float32)
    with_sin = jnp.einsum("kn,lrkm->lnrm", sin_table, values, preferred_element_type=jnp.float32)
    real_part = with_cos[:, :, 0] - with_sin[:, :, 1]
    imag_part = with_cos[:, :, 1] + with_sin[:, :, 0]
    return jnp.stack([real_part, imag_part], axis=2)


def spectral_apply(weights, mode_values):
    wide = weights.astype(jnp.float32)
    real_mode = mode_values[:, 0].astype(jnp.float32)
    imag_mode = mode_values[:, 1].astype(jnp.float32)
    for_real = jnp.stack([real_mode, -imag_mode], axis=0)[:, :, None]
    for_imag = jnp.stack([imag_mode, real_mode], axis=0)[:, :, None]
    out_real = jnp.sum(wide * for_real, axis=(0, 1))
    out_imag = jnp.sum(wide * for_imag, axis=(0, 1))
    return jnp.stack([out_real, out_imag], axis=1).astype(jnp.bfloat16)


def spectral_adjoint(weights, mode_values, upstream_modes):
    wide = weights.astype(jnp.float32)
    real_mode = mode_values[:, 0].astype(jnp.float32)
    imag_mode = mode_values[:, 1].astype(jnp.float32)
    real_up = upstream_modes[:, 0].astype(jnp.float32)
    imag_up = upstream_modes[:, 1].astype(jnp.float32)
    grad_real = real_up[None] * real_mode[:, None] + imag_up[None] * imag_mode[:, None]
    grad_imag = imag_up[None] * real_mode[:, None] - real_up[None] * imag_mode[:, None]
    for_real = jnp.stack([real_up, imag_up], axis=0)[:, None]
    for_imag = jnp.stack([imag_up, -real_up], axis=0)[:, None]
    back_real = jnp.sum(wide * for_real, axis=(0, 2))
    back_imag = jnp.sum(wide * for_imag, axis=(0, 2))
    return (jnp.stack([grad_real, grad_imag], axis=0), jnp.stack([back_real, back_imag], axis=1))


def gelu_slope(values):
    return (
        0.5 * (1.0 + lax.erf(values * 0.7071067811865476))
        + values * jnp.exp(-0.5 * values * values) * 0.3989422804014327
    )


def local(field, cotangent, spectral_weight, local_weight, bias):
    channels, width_x, width_y, depth_cells = field.shape
    kept_plane = MS * MT
    plane_table = plane_tables(NZ, NT, MS, MT)
    local_rows = lax.axis_index("gy") * width_y + jnp.arange(width_y, dtype=jnp.int32)
    cos_local, sin_local = axis_tables(NY, MS, local_rows)
    cos_across, sin_across = axis_tables(NX, MS, jnp.arange(NX, dtype=jnp.int32))

    plane_cos = plane_table[:, :kept_plane]
    plane_sin = plane_table[:, kept_plane:]
    forward_real = jnp.stack([cos_local, -sin_local], axis=0)
    forward_imag = jnp.stack([sin_local, cos_local], axis=0)

    def forward_chain(planes):
        flat = planes.reshape(-1, depth_cells)
        lead = channels * width_x

        def plane_part(table):
            part = jnp.dot(flat, table, preferred_element_type=jnp.float32)
            return part.astype(jnp.bfloat16).reshape(lead, width_y, kept_plane)

        real, imag = plane_part(plane_cos), plane_part(plane_sin)
        partial_terms = jnp.einsum(
            "pkn,lnm->lpkm", forward_real, real, preferred_element_type=jnp.float32
        ) + jnp.einsum("pkn,lnm->lpkm", forward_imag, imag, preferred_element_type=jnp.float32)
        partial_terms = partial_terms.astype(jnp.bfloat16)
        groups = lax.axis_size("gy")
        lead, parts, kept_rows, plane = partial_terms.shape
        pieces = partial_terms.reshape(lead, parts, groups, kept_rows // groups, plane)
        pieces = lax.all_to_all(pieces, "gy", split_axis=2, concat_axis=2, tiled=True)
        row_modes = jnp.sum(pieces.astype(jnp.float32), axis=2).astype(jnp.bfloat16)
        row_modes = row_modes.reshape(channels, width_x, 2, -1)
        blocks = lax.all_to_all(row_modes, "gx", split_axis=3, concat_axis=1, tiled=True)
        return forward_axis(blocks, cos_across, sin_across).astype(jnp.bfloat16)

    def inverse_chain(mode_values):
        across = inverse_axis(mode_values, cos_across, sin_across).astype(jnp.bfloat16)
        row_modes = lax.all_to_all(across, "gx", split_axis=1, concat_axis=3, tiled=True)
        row_modes = row_modes.reshape(channels * width_x, 2, -1, kept_plane)
        all_rows = lax.all_gather(row_modes, "gy", axis=2, tiled=True)
        summed = 0.0
        for rows_table, table in ((forward_real, plane_cos), (forward_imag, plane_sin)):
            part = jnp.einsum("pkn,lpkm->lnm", rows_table, all_rows, preferred_element_type=jnp.float32)
            part = part.astype(jnp.bfloat16).reshape(-1, kept_plane)
            summed = summed + lax.dot_general(
                part, table, (((1,), (1,)), ((), ())), preferred_element_type=jnp.float32
            )
        return summed.reshape(field.shape)

    field_modes = forward_chain(field)
    mixed_modes = spectral_apply(spectral_weight, field_modes)
    spectral = inverse_chain(mixed_modes)
    direct = jnp.einsum("io,ixyp->oxyp", local_weight, field, preferred_element_type=jnp.float32)
    before = spectral + direct + bias[:, None, None, None]
    upstream = (cotangent.astype(jnp.float32) * gelu_slope(before)).astype(jnp.bfloat16)
    upstream_modes = forward_chain(upstream)
    grad_weight, back_modes = spectral_adjoint(spectral_weight, field_modes, upstream_modes)
    returned = inverse_chain(back_modes.astype(jnp.bfloat16))
    direct_back = jnp.einsum(
        "io,oxyp->ixyp", local_weight, upstream, preferred_element_type=jnp.float32
    )
    return ((returned + direct_back).astype(jnp.bfloat16), grad_weight)


def solution(mesh):
    in_specs = (
        P(None, "gx", "gy", None),
        P(None, "gx", "gy", None),
        P(None, None, None, None, ("gy", "gx")),
        P(),
        P(),
    )
    out_specs = (P(None, "gx", "gy", None), P(None, None, None, None, ("gy", "gx")))
    return jax.shard_map(local, mesh=mesh, in_specs=in_specs, out_specs=out_specs, check_vma=False)
```

```python
import math

import jax
import jax.numpy as jnp
from jax import lax
from jax.sharding import PartitionSpec as P

NX = 128
NY = 128
NZ = 128
NT = 8
MS = 24
MT = 8


def axis_tables(length, kept_count, positions):
    half_kept = kept_count // 2
    mode_index = jnp.arange(kept_count, dtype=jnp.int32)
    frequency = jnp.where(mode_index < half_kept, mode_index, mode_index - kept_count)
    phases = jnp.mod(frequency[:, None] * positions[None, :], length)
    angles = phases.astype(jnp.float32) * (2.0 * math.pi / length)
    factor = 1.0 / math.sqrt(length)
    return (
        (jnp.cos(angles) * factor).astype(jnp.bfloat16),
        (jnp.sin(angles) * factor).astype(jnp.bfloat16),
    )


def plane_tables(depth_cells, time_steps, kept_count, kept_time):
    period = depth_cells * time_steps
    kept_plane = kept_count * kept_time
    depth_cos, depth_sin = unit_circle(depth_cells, kept_count, depth_cells, True)
    time_cos, time_sin = unit_circle(time_steps, kept_time, time_steps, False)

    def spread(depth_part, time_part):
        depth_wide = jnp.broadcast_to(
            depth_part[:, :, None], (depth_cells, kept_count, kept_time)
        ).reshape(depth_cells, 1, kept_plane)
        time_wide = jnp.broadcast_to(
            time_part[:, None, :], (time_steps, kept_count, kept_time)
        ).reshape(1, time_steps, kept_plane)
        return depth_wide, time_wide

    zc, tc = spread(depth_cos, time_cos)
    zs, ts = spread(depth_sin, time_sin)
    factor = 1.0 / math.sqrt(period)
    cos_sum = (zc * tc - zs * ts) * factor
    sin_sum = (zs * tc + zc * ts) * (-factor)
    table = jnp.concatenate([cos_sum, sin_sum], axis=2)
    return table.reshape(period, 2 * kept_plane).astype(jnp.bfloat16)


def unit_circle(length, kept_count, cells, centred):
    mode_index = jnp.arange(kept_count, dtype=jnp.int32)
    if centred:
        frequency = jnp.where(mode_index < kept_count // 2, mode_index, mode_index - kept_count)
    else:
        frequency = mode_index
    positions = jnp.arange(cells, dtype=jnp.int32)
    phases = jnp.mod(positions[:, None] * frequency[None, :], length)
    angles = phases.astype(jnp.float32) * (2.0 * math.pi / length)
    return jnp.cos(angles), jnp.sin(angles)


def forward_axis(values, cos_table, sin_table):
    with_cos = jnp.einsum("kn,lnrm->lrkm", cos_table, values, preferred_element_type=jnp.float32)
    with_sin = jnp.einsum("kn,lnrm->lrkm", sin_table, values, preferred_element_type=jnp.float32)
    real_part = with_cos[:, 0] + with_sin[:, 1]
    imag_part = with_cos[:, 1] - with_sin[:, 0]
    return jnp.stack([real_part, imag_part], axis=1)


def inverse_axis(values, cos_table, sin_table):
    with_cos = jnp.einsum("kn,lrkm->lnrm", cos_table, values, preferred_element_type=jnp.float32)
    with_sin = jnp.einsum("kn,lrkm->lnrm", sin_table, values, preferred_element_type=jnp.float32)
    real_part = with_cos[:, :, 0] - with_sin[:, :, 1]
    imag_part = with_cos[:, :, 1] + with_sin[:, :, 0]
    return jnp.stack([real_part, imag_part], axis=2)


def spectral_apply(weights, mode_values):
    real_weight = weights[0].astype(jnp.float32)
    imag_weight = weights[1].astype(jnp.float32)
    real_mode = mode_values[:, 0].astype(jnp.float32)[:, None]
    imag_mode = mode_values[:, 1].astype(jnp.float32)[:, None]
    out_real = jnp.sum(real_weight * real_mode - imag_weight * imag_mode, axis=0)
    out_imag = jnp.sum(real_weight * imag_mode + imag_weight * real_mode, axis=0)
    return jnp.stack([out_real, out_imag], axis=1).astype(jnp.bfloat16)


def spectral_adjoint(weights, mode_values, upstream_modes):
    real_weight = weights[0].astype(jnp.float32)
    imag_weight = weights[1].astype(jnp.float32)
    real_mode = mode_values[:, 0].astype(jnp.float32)
    imag_mode = mode_values[:, 1].astype(jnp.float32)
    real_up = upstream_modes[:, 0].astype(jnp.float32)
    imag_up = upstream_modes[:, 1].astype(jnp.float32)
    grad_real = real_up[None] * real_mode[:, None] + imag_up[None] * imag_mode[:, None]
    grad_imag = imag_up[None] * real_mode[:, None] - real_up[None] * imag_mode[:, None]
    back_real = jnp.sum(real_weight * real_up[None] + imag_weight * imag_up[None], axis=1)
    back_imag = jnp.sum(real_weight * imag_up[None] - imag_weight * real_up[None], axis=1)
    return (jnp.stack([grad_real, grad_imag], axis=0), jnp.stack([back_real, back_imag], axis=1))


def gelu_slope(values):
    return (
        0.5 * (1.0 + lax.erf(values * 0.7071067811865476))
        + values * jnp.exp(-0.5 * values * values) * 0.3989422804014327
    )


def local(field, cotangent, spectral_weight, local_weight, bias):
    channels, width_x, width_y, depth_cells = field.shape
    kept_plane = MS * MT
    plane_table = plane_tables(NZ, NT, MS, MT)
    local_rows = lax.axis_index("gy") * width_y + jnp.arange(width_y, dtype=jnp.int32)
    cos_local, sin_local = axis_tables(NY, MS, local_rows)
    cos_across, sin_across = axis_tables(NX, MS, jnp.arange(NX, dtype=jnp.int32))

    plane_cos = plane_table[:, :kept_plane]
    plane_sin = plane_table[:, kept_plane:]
    forward_real = jnp.stack([cos_local, -sin_local], axis=0)
    forward_imag = jnp.stack([sin_local, cos_local], axis=0)

    def forward_chain(planes):
        flat = planes.reshape(-1, depth_cells)
        lead = channels * width_x

        def plane_part(table):
            part = jnp.dot(flat, table, preferred_element_type=jnp.float32)
            return part.astype(jnp.bfloat16).reshape(lead, width_y, kept_plane)

        real, imag = plane_part(plane_cos), plane_part(plane_sin)
        partial_terms = jnp.einsum(
            "pkn,lnm->pklm", forward_real, real, preferred_element_type=jnp.float32
        ) + jnp.einsum("pkn,lnm->pklm", forward_imag, imag, preferred_element_type=jnp.float32)
        partial_terms = partial_terms.astype(jnp.bfloat16)
        groups = lax.axis_size("gy")
        parts, kept_rows, lead, plane = partial_terms.shape
        pieces = partial_terms.reshape(parts, groups, kept_rows // groups, lead, plane)
        pieces = lax.all_to_all(pieces, "gy", split_axis=1, concat_axis=1, tiled=True)
        row_modes = jnp.sum(pieces.astype(jnp.float32), axis=1).astype(jnp.bfloat16)
        row_modes = jnp.transpose(row_modes, (2, 0, 1, 3)).reshape(channels, width_x, 2, -1)
        blocks = lax.all_to_all(row_modes, "gx", split_axis=3, concat_axis=1, tiled=True)
        return forward_axis(blocks, cos_across, sin_across).astype(jnp.bfloat16)

    def inverse_chain(mode_values):
        across = inverse_axis(mode_values, cos_across, sin_across).astype(jnp.bfloat16)
        row_modes = lax.all_to_all(across, "gx", split_axis=1, concat_axis=3, tiled=True)
        row_modes = row_modes.reshape(channels * width_x, 2, -1, kept_plane)
        all_rows = lax.all_gather(row_modes, "gy", axis=2, tiled=True)
        summed = 0.0
        for rows_table, table in ((forward_real, plane_cos), (forward_imag, plane_sin)):
            part = jnp.einsum("pkn,lpkm->lnm", rows_table, all_rows, preferred_element_type=jnp.float32)
            part = part.astype(jnp.bfloat16).reshape(-1, kept_plane)
            summed = summed + lax.dot_general(
                part, table, (((1,), (1,)), ((), ())), preferred_element_type=jnp.float32
            )
        return summed.reshape(field.shape)

    field_modes = forward_chain(field)
    mixed_modes = spectral_apply(spectral_weight, field_modes)
    spectral = inverse_chain(mixed_modes)
    direct = jnp.einsum("io,ixyp->oxyp", local_weight, field, preferred_element_type=jnp.float32)
    before = spectral + direct + bias[:, None, None, None]
    upstream = (cotangent.astype(jnp.float32) * gelu_slope(before)).astype(jnp.bfloat16)
    upstream_modes = forward_chain(upstream)
    grad_weight, back_modes = spectral_adjoint(spectral_weight, field_modes, upstream_modes)
    returned = inverse_chain(back_modes.astype(jnp.bfloat16))
    direct_back = jnp.einsum(
        "io,oxyp->ixyp", local_weight, upstream, preferred_element_type=jnp.float32
    )
    return ((returned + direct_back).astype(jnp.bfloat16), grad_weight)


def solution(mesh):
    in_specs = (
        P(None, "gx", "gy", None),
        P(None, "gx", "gy", None),
        P(None, None, None, None, ("gy", "gx")),
        P(),
        P(),
    )
    out_specs = (P(None, "gx", "gy", None), P(None, None, None, None, ("gy", "gx")))
    return jax.shard_map(local, mesh=mesh, in_specs=in_specs, out_specs=out_specs, check_vma=False)
```

```python
import math

import jax
import jax.numpy as jnp
from jax import lax
from jax.sharding import PartitionSpec as P

NX = 128
NY = 128
NZ = 128
NT = 8
MS = 24
MT = 8


def axis_tables(length, kept_count, positions):
    half_kept = kept_count // 2
    mode_index = jnp.arange(kept_count, dtype=jnp.int32)
    frequency = jnp.where(mode_index < half_kept, mode_index, mode_index - kept_count)
    phases = jnp.mod(frequency[:, None] * positions[None, :], length)
    angles = phases.astype(jnp.float32) * (2.0 * math.pi / length)
    factor = 1.0 / math.sqrt(length)
    return (
        (jnp.cos(angles) * factor).astype(jnp.bfloat16),
        (jnp.sin(angles) * factor).astype(jnp.bfloat16),
    )


def plane_tables(depth_cells, time_steps, kept_count, kept_time):
    period = depth_cells * time_steps
    kept_plane = kept_count * kept_time
    depth_cos, depth_sin = unit_circle(depth_cells, kept_count, depth_cells, True)
    time_cos, time_sin = unit_circle(time_steps, kept_time, time_steps, False)

    def spread(depth_part, time_part):
        depth_wide = jnp.broadcast_to(
            depth_part[:, :, None], (depth_cells, kept_count, kept_time)
        ).reshape(depth_cells, 1, kept_plane)
        time_wide = jnp.broadcast_to(
            time_part[:, None, :], (time_steps, kept_count, kept_time)
        ).reshape(1, time_steps, kept_plane)
        return depth_wide, time_wide

    zc, tc = spread(depth_cos, time_cos)
    zs, ts = spread(depth_sin, time_sin)
    factor = 1.0 / math.sqrt(period)
    cos_sum = (zc * tc - zs * ts) * factor
    sin_sum = (zs * tc + zc * ts) * (-factor)
    table = jnp.concatenate([cos_sum, sin_sum], axis=2)
    return table.reshape(period, 2 * kept_plane).astype(jnp.bfloat16)


def unit_circle(length, kept_count, cells, centred):
    mode_index = jnp.arange(kept_count, dtype=jnp.int32)
    if centred:
        frequency = jnp.where(mode_index < kept_count // 2, mode_index, mode_index - kept_count)
    else:
        frequency = mode_index
    positions = jnp.arange(cells, dtype=jnp.int32)
    phases = jnp.mod(positions[:, None] * frequency[None, :], length)
    angles = phases.astype(jnp.float32) * (2.0 * math.pi / length)
    return jnp.cos(angles), jnp.sin(angles)


def forward_axis(values, cos_table, sin_table):
    with_cos = jnp.einsum("kn,lnrm->lrkm", cos_table, values, preferred_element_type=jnp.float32)
    with_sin = jnp.einsum("kn,lnrm->lrkm", sin_table, values, preferred_element_type=jnp.float32)
    real_part = with_cos[:, 0] + with_sin[:, 1]
    imag_part = with_cos[:, 1] - with_sin[:, 0]
    return jnp.stack([real_part, imag_part], axis=1)


def inverse_axis(values, cos_table, sin_table):
    with_cos = jnp.einsum("kn,lrkm->lnrm", cos_table, values, preferred_element_type=jnp.float32)
    with_sin = jnp.einsum("kn,lrkm->lnrm", sin_table, values, preferred_element_type=jnp.float32)
    real_part = with_cos[:, :, 0] - with_sin[:, :, 1]
    imag_part = with_cos[:, :, 1] + with_sin[:, :, 0]
    return jnp.stack([real_part, imag_part], axis=2)


def spectral_apply(weights, mode_values):
    real_weight = weights[0].astype(jnp.float32)
    imag_weight = weights[1].astype(jnp.float32)
    real_mode = mode_values[:, 0].astype(jnp.float32)[:, None]
    imag_mode = mode_values[:, 1].astype(jnp.float32)[:, None]
    out_real = jnp.sum(real_weight * real_mode - imag_weight * imag_mode, axis=0)
    out_imag = jnp.sum(real_weight * imag_mode + imag_weight * real_mode, axis=0)
    return jnp.stack([out_real, out_imag], axis=1).astype(jnp.bfloat16)


def spectral_adjoint(weights, mode_values, upstream_modes):
    real_weight = weights[0].astype(jnp.float32)
    imag_weight = weights[1].astype(jnp.float32)
    real_mode = mode_values[:, 0].astype(jnp.float32)
    imag_mode = mode_values[:, 1].astype(jnp.float32)
    real_up = upstream_modes[:, 0].astype(jnp.float32)
    imag_up = upstream_modes[:, 1].astype(jnp.float32)
    grad_real = real_up[None] * real_mode[:, None] + imag_up[None] * imag_mode[:, None]
    grad_imag = imag_up[None] * real_mode[:, None] - real_up[None] * imag_mode[:, None]
    back_real = jnp.sum(real_weight * real_up[None] + imag_weight * imag_up[None], axis=1)
    back_imag = jnp.sum(real_weight * imag_up[None] - imag_weight * real_up[None], axis=1)
    return (jnp.stack([grad_real, grad_imag], axis=0), jnp.stack([back_real, back_imag], axis=1))


def gelu_slope(values):
    return (
        0.5 * (1.0 + lax.erf(values * 0.7071067811865476))
        + values * jnp.exp(-0.5 * values * values) * 0.3989422804014327
    )


def local(field, cotangent, spectral_weight, local_weight, bias):
    channels, width_x, width_y, depth_cells = field.shape
    kept_plane = MS * MT
    plane_table = plane_tables(NZ, NT, MS, MT)
    local_rows = lax.axis_index("gy") * width_y + jnp.arange(width_y, dtype=jnp.int32)
    cos_local, sin_local = axis_tables(NY, MS, local_rows)
    cos_across, sin_across = axis_tables(NX, MS, jnp.arange(NX, dtype=jnp.int32))

    plane_cos = plane_table[:, :kept_plane]
    plane_sin = plane_table[:, kept_plane:]
    forward_real = jnp.stack([cos_local, -sin_local], axis=0)
    forward_imag = jnp.stack([sin_local, cos_local], axis=0)

    def forward_chain(planes):
        flat = planes.reshape(-1, depth_cells)
        lead = channels * width_x

        def plane_part(table):
            part = lax.dot_general(
                table, flat, (((0,), (1,)), ((), ())), preferred_element_type=jnp.float32
            )
            return part.astype(jnp.bfloat16).reshape(kept_plane, lead, width_y)

        real, imag = plane_part(plane_cos), plane_part(plane_sin)
        partial_terms = jnp.einsum(
            "pkn,mln->pklm", forward_real, real, preferred_element_type=jnp.float32
        ) + jnp.einsum("pkn,mln->pklm", forward_imag, imag, preferred_element_type=jnp.float32)
        partial_terms = partial_terms.astype(jnp.bfloat16)
        groups = lax.axis_size("gy")
        parts, kept_rows, lead, plane = partial_terms.shape
        pieces = partial_terms.reshape(parts, groups, kept_rows // groups, lead, plane)
        pieces = lax.all_to_all(pieces, "gy", split_axis=1, concat_axis=1, tiled=True)
        row_modes = jnp.sum(pieces.astype(jnp.float32), axis=1).astype(jnp.bfloat16)
        row_modes = jnp.transpose(row_modes, (2, 0, 1, 3)).reshape(channels, width_x, 2, -1)
        blocks = lax.all_to_all(row_modes, "gx", split_axis=3, concat_axis=1, tiled=True)
        return forward_axis(blocks, cos_across, sin_across).astype(jnp.bfloat16)

    def inverse_chain(mode_values):
        across = inverse_axis(mode_values, cos_across, sin_across).astype(jnp.bfloat16)
        row_modes = lax.all_to_all(across, "gx", split_axis=1, concat_axis=3, tiled=True)
        row_modes = row_modes.reshape(channels * width_x, 2, -1, kept_plane)
        all_rows = lax.all_gather(row_modes, "gy", axis=2, tiled=True)
        summed = 0.0
        for rows_table, table in ((forward_real, plane_cos), (forward_imag, plane_sin)):
            part = jnp.einsum("pkn,lpkm->lnm", rows_table, all_rows, preferred_element_type=jnp.float32)
            part = part.astype(jnp.bfloat16).reshape(-1, kept_plane)
            summed = summed + lax.dot_general(
                part, table, (((1,), (1,)), ((), ())), preferred_element_type=jnp.float32
            )
        return summed.reshape(field.shape)

    field_modes = forward_chain(field)
    mixed_modes = spectral_apply(spectral_weight, field_modes)
    spectral = inverse_chain(mixed_modes)
    direct = jnp.einsum("io,ixyp->oxyp", local_weight, field, preferred_element_type=jnp.float32)
    before = spectral + direct + bias[:, None, None, None]
    upstream = (cotangent.astype(jnp.float32) * gelu_slope(before)).astype(jnp.bfloat16)
    upstream_modes = forward_chain(upstream)
    grad_weight, back_modes = spectral_adjoint(spectral_weight, field_modes, upstream_modes)
    returned = inverse_chain(back_modes.astype(jnp.bfloat16))
    direct_back = jnp.einsum(
        "io,oxyp->ixyp", local_weight, upstream, preferred_element_type=jnp.float32
    )
    return ((returned + direct_back).astype(jnp.bfloat16), grad_weight)


def solution(mesh):
    in_specs = (
        P(None, "gx", "gy", None),
        P(None, "gx", "gy", None),
        P(None, None, None, None, ("gy", "gx")),
        P(),
        P(),
    )
    out_specs = (P(None, "gx", "gy", None), P(None, None, None, None, ("gy", "gx")))
    return jax.shard_map(local, mesh=mesh, in_specs=in_specs, out_specs=out_specs, check_vma=False)
```
